32 devices in a mesh: group: 2 (over x), span: 16 (over z, y, core).
Axes of the slice: x: 2, y: 2, z: 4, core: 2. Of those that a mesh axis runs over, the one named last changes fastest.
Arguments:
- queries: bfloat16 [8192, 2560], P(('group', 'span')), parts along dimension 0, may hold values from -6 to 6
- keys_values: bfloat16 [2, 8192, 2560], P(None, ('group', 'span')), parts along dimension 1, may hold values from -6 to 6
- owner: int32 [2], P('group'), parts along dimension 0, may hold values from 0 to 15
- span_mask: int32 [32, 3], P('group'), parts along dimension 0, may hold values 0 or 1
- lengths: int32 [32], P('group'), parts along dimension 0, may hold values from 128 to 256, as said below
- frames: bfloat16 [6, 16, 52, 384], P('group', 'span'), parts along dimension 0, may hold values from -6 to 6
- past_frames: bfloat16 [4, 16, 52, 384], P('group', 'span'), parts along dimension 0, may hold values from -5 to 5
- norm_gain: float32 [384], replicated, may hold values from 0.5 to 1.5
- conv_weight: bfloat16 [3, 3, 3, 384, 384], replicated, may hold values from -0.0625 to 0.0625
- conv_bias: float32 [384], replicated, may hold values from -3 to 3
Outputs:
- attended: bfloat16 [8192, 2560], P(('group', 'span')), parts along dimension 0
- decoded: bfloat16 [6, 16, 52, 384], P('group', 'span'), parts along dimension 0
The draws below stay inside these ranges and needn't reach their ends.
There are 2 independent parts, one for each index of `group`. The reference program is written for one: setup_inputs(seed, part) draws one part's arguments, and reference() takes and returns one part's arrays. A program takes and returns all parts, laid end to end along the dimension named above; an argument that names none is the same for every part. Nothing has to cross between parts.
Inputs may be any that keep to these rules, and one draw needn't show every extreme that they name: `lengths`: at least one slot holds exactly 256 tokens.
All inputs are finite; a program needn't handle non-finite values.
Results may differ from the reference program's by a relative error of at most 0.005.
Values may be sent and summed in bfloat16 or wider, within the bound.
No kernel may reach another device: no remote copies, remote signals or barrier semaphores. Data moves between devices by JAX's collectives and lax.ppermute only.
A program may use at most 128 MiB of HBM per device.

```python
import jax
import jax.numpy as jnp
from jax import lax

H = 20
DH = 128
CH = 256
WIN = 4
C = 384
FRAMES = 3
PAST = 2
COLS = 52
SPANS = 16
TOKENS = 4096
ROWS = 16


def base_values(key, shape):
    return jnp.clip(1.5 * jax.random.normal(key, shape, jnp.float32), -6.0, 6.0)


def draw_queries(key, part):
    values = base_values(jax.random.fold_in(key, 1), (SPANS, CH, H * DH))
    return values.reshape(SPANS * CH, H * DH).astype(jnp.bfloat16)


def draw_keys_values(key, part):
    key_part = base_values(jax.random.fold_in(key, 2), (SPANS, CH, H * DH))
    value_part = base_values(jax.random.fold_in(key, 3), (SPANS, CH, H * DH))
    stacked = jnp.stack([key_part, value_part]).reshape(2, SPANS * CH, H * DH)
    return stacked.astype(jnp.bfloat16)


def draw_lengths(key, part):
    token_counts = jax.random.randint(jax.random.fold_in(key, 5), (SPANS,), CH // 2, CH + 1)
    longest = jax.random.randint(jax.random.fold_in(key, 6), (), 0, SPANS)
    return jnp.where(jnp.arange(SPANS) == longest, CH, token_counts).astype(jnp.int32)


def place_ends(values, stream_key, least, largest):
    extent = values.shape
    spot = [jax.random.randint(jax.random.fold_in(stream_key, axis), (), 0, extent[axis]) for axis in range(len(extent))]
    values = values.at[tuple(spot)].set(least)
    longest = extent.index(max(extent))
    spot[longest] = (spot[longest] + 1) % extent[longest]
    return values.at[tuple(spot)].set(largest)


def block_levels(key, shape, pieces, low, high):
    loudness = 1.0
    for axis_at, parts in pieces:
        draws = jax.random.uniform(jax.random.fold_in(jax.random.fold_in(key, 6), axis_at), (parts,), jnp.float32, low / len(pieces), high / len(pieces))
        loudness = loudness * jnp.repeat(jnp.exp(draws), shape[axis_at] // parts).reshape((-1,) + (1,) * (len(shape) - 1 - axis_at))
    return loudness


def normal_values(stream_key, dims, scale, bound, split=(), held_as=jnp.bfloat16):
    entries = scale * jax.random.normal(stream_key, dims, jnp.float32)
    if split:
        entries = entries * block_levels(stream_key, dims, split, -0.22, 0.18)
    return jnp.clip(entries, -bound, bound).astype(held_as)


def setup_inputs(seed: int = 0, part: int = 0) -> dict:
    streams_of = jax.random.split(jax.random.key(seed), 11)
    part_splits = jax.random.split(jax.random.fold_in(streams_of[10], part), 11)
    return {
        "queries": draw_queries(jax.random.fold_in(jax.random.fold_in(streams_of[10], part), 71), part),
        "keys_values": draw_keys_values(jax.random.fold_in(jax.random.fold_in(streams_of[10], part), 71), part),
        "owner": jax.random.randint(part_splits[2], (1,), 0, SPANS).astype(jnp.int32),
        "span_mask": place_ends((jax.random.randint(part_splits[3], (SPANS, WIN - 1), 0, 4) < 3).astype(jnp.int32), jax.random.fold_in(part_splits[3], 1), 0, 1),
        "lengths": draw_lengths(jax.random.fold_in(jax.random.fold_in(streams_of[10], part), 71), part),
        "frames": normal_values(part_splits[5], (FRAMES, ROWS, COLS, C), 1.0, 6.0, ((1, 16),)),
        "past_frames": normal_values(part_splits[6], (PAST, ROWS, COLS, C), 0.7, 5.0, ((1, 16),)),
        "norm_gain": jnp.clip(1.0 + 0.1 * jax.random.normal(streams_of[7], (C,), jnp.float32), 0.5, 1.5),
        "conv_weight": normal_values(streams_of[8], (3, 3, 3, C, C), (27 * C) ** -0.5, 0.0625),
        "conv_bias": normal_values(streams_of[9], (C,), 0.5, 3.0, (), jnp.float32),
    }


def reference(queries, keys_values, owner, span_mask, lengths, frames, past_frames, norm_gain, conv_weight, conv_bias):
    anchor = owner[0]
    row_ids = jnp.arange(CH, dtype=jnp.int32)
    score_scale = DH ** (-0.5)

    def one_span(place):
        position = (place - anchor - 1) % SPANS
        query_rows = lax.dynamic_slice_in_dim(queries, (place * CH).astype(jnp.int32), CH, 0)
        blocks = []
        valid_list = []
        for offset in range(WIN):
            source = ((place - offset) % SPANS).astype(jnp.int32)
            blocks.append(lax.dynamic_slice_in_dim(keys_values, source * CH, CH, 1))
            if offset == 0:
                allowed = jnp.array(True)
            else:
                allowed = (position >= offset) & (span_mask[position, offset - 1] == 1)
            valid_list.append(allowed & (row_ids < lengths[source]))
        blocks.append(lax.dynamic_slice_in_dim(keys_values, (anchor * CH).astype(jnp.int32), CH, 1))
        valid_list.append((place != anchor) & (row_ids < lengths[anchor]))
        gathered = jnp.concatenate(blocks, axis=1)
        key_valid = jnp.concatenate(valid_list)
        query_heads = query_rows.reshape(CH, H, DH).astype(jnp.float32)
        key_heads = gathered[0].reshape(-1, H, DH).astype(jnp.float32)
        value_heads = gathered[1].reshape(-1, H, DH).astype(jnp.float32)
        scores = jnp.einsum('qhd,khd->hqk', query_heads, key_heads) * score_scale
        scores = jnp.where(key_valid[None, None, :], scores, -jnp.inf)
        row_max = lax.optimization_barrier(jnp.max(scores, axis=-1, keepdims=True))
        weights = jnp.exp(scores - row_max)
        probs = (weights / lax.optimization_barrier(jnp.sum(weights, axis=-1, keepdims=True))).astype(jnp.bfloat16)
        blended = jnp.einsum('hqk,khd->qhd', probs.astype(jnp.float32), value_heads).reshape(CH, H * DH)
        blended = jnp.where(row_ids[:, None] < lengths[place], blended, 0.0)
        return blended.astype(jnp.bfloat16)
    attended = lax.map(one_span, jnp.arange(SPANS, dtype=jnp.int32)).reshape(TOKENS, H * DH)
    features = frames.astype(jnp.float32)
    squares = lax.optimization_barrier(jnp.mean(features * features, axis=-1, keepdims=True))
    normed = features * lax.rsqrt(squares + 1e-06) * norm_gain
    activated = jax.nn.silu(normed).astype(jnp.bfloat16)
    stacked = jnp.concatenate([past_frames, activated], axis=0)
    padded = jnp.pad(stacked, ((0, 0), (1, 1), (1, 1), (0, 0)))
    windows = []
    for frame_tap in range(3):
        for row_tap in range(3):
            for col_tap in range(3):
                windows.append(padded[frame_tap:frame_tap + FRAMES, row_tap:row_tap + ROWS, col_tap:col_tap + COLS, :])
    columns = jnp.concatenate(windows, axis=-1).reshape(-1, 27 * C)
    convolved = jnp.dot(columns, conv_weight.reshape(27 * C, C), preferred_element_type=jnp.float32)
    decoded = features + conv_bias + convolved.reshape(FRAMES, ROWS, COLS, C)
    return (attended, decoded.astype(jnp.bfloat16))
```

```python
import jax
import jax.numpy as jnp
from jax import lax
from jax.sharding import PartitionSpec as P

H = 20
DH = 128
WIN = 4


def spread(block, axis, source):
    block = jnp.where(lax.axis_index(axis) == source, block, jnp.zeros_like(block))
    return lax.psum(block, axis)


def extended_2(block, sides, width):
    for axis, dim in sides:
        count = lax.axis_size(axis)
        forward = [(i, i + 1) for i in range(count - 1)]
        backward = [(target, source) for source, target in forward]
        low = lax.ppermute(
            lax.slice_in_dim(block, block.shape[dim] - width, None, axis=dim), axis, forward
        )
        high = lax.ppermute(lax.slice_in_dim(block, 0, width, axis=dim), axis, backward)
        block = jnp.concatenate([low, block, high], axis=dim)
    return block


def move(value, pairs):
    return lax.ppermute(value, "span", pairs)


def window_blocks(kv, devices):
    rows = devices // 4
    lane = lax.axis_index("span") % 4

    def at(r, l):
        return 4 * (r % rows) + l

    rng = range(rows)
    rail1 = move(kv, [(at(r, 3), at(r + 1, 2)) for r in rng])
    rail0 = move(kv, [(at(r, 1), at(r + 1, 0)) for r in rng])
    y_up = move(kv, [(at(r, 0), at(r, 2)) for r in rng] + [(at(r, 1), at(r, 3)) for r in rng])
    y_down = move(kv, [(at(r, 2), at(r, 1)) for r in rng])
    chip = move(kv, [(at(r, 0), at(r, 1)) for r in rng] + [(at(r, 2), at(r, 3)) for r in rng])
    swap = move(y_up, [(at(r, 3), at(r, 2)) for r in rng] + [(at(r, 2), at(r, 3)) for r in rng])
    down2 = move(rail1, [(at(r, 2), at(r, 0)) for r in rng])
    rail0b = move(y_down, [(at(r, 1), at(r + 1, 0)) for r in rng])
    pair = move(jnp.stack([down2, rail0b]), [(at(r, 0), at(r, 1)) for r in rng])

    def pick(*options):
        out = options[0]
        for l in range(1, 4):
            out = jnp.where(lane == l, options[l], out)
        return out

    b1 = pick(down2, chip, swap, chip)
    b2 = pick(rail0b, pair[0], y_up, y_up)
    b3 = pick(rail0, pair[1], rail1, swap)
    return b1, b2, b3


def part_stats(q, k, valid, scale):
    scores = jnp.einsum("qhd,khd->hqk", q, k, preferred_element_type=jnp.float32) * scale
    return jnp.where(valid[None, None, :], scores, -jnp.inf)


def shards(
    queries,
    keys_values,
    owner,
    span_mask,
    lengths,
    frames,
    past_frames,
    norm_gain,
    conv_weight,
    conv_bias,
):
    devices = lax.axis_size("span")
    place = lax.axis_index("span")
    anchor = owner[0]
    position = (place - anchor - 1) % devices
    tok_rows = queries.shape[0]
    row_ids = jnp.arange(tok_rows, dtype=jnp.int32)
    anchor_kv = spread(keys_values, "span", anchor)
    b1, b2, b3 = window_blocks(keys_values, devices)
    blocks = [keys_values, b1, b2, b3]
    valid_list = [row_ids < lengths[place]]
    for offset in range(1, WIN):
        source = (place - offset) % devices
        allowed = (position >= offset) & (span_mask[position, offset - 1] == 1)
        valid_list.append(allowed & (row_ids < lengths[source]))
    anchor_valid = (place != anchor) & (row_ids < lengths[anchor])
    window_kv = jnp.concatenate(blocks, axis=1)
    window_valid = jnp.concatenate(valid_list)
    score_scale = DH ** (-0.5)
    pieces = []
    for head_block in range(H // 4):
        first_col = head_block * 4 * DH
        last_col = first_col + 4 * DH
        q = queries[:, first_col:last_col].reshape(tok_rows, 4, DH)
        wk = window_kv[0, :, first_col:last_col].reshape(-1, 4, DH)
        wv = window_kv[1, :, first_col:last_col].reshape(-1, 4, DH)
        ak = anchor_kv[0, :, first_col:last_col].reshape(-1, 4, DH)
        av = anchor_kv[1, :, first_col:last_col].reshape(-1, 4, DH)
        ws = part_stats(q, wk, window_valid, score_scale)
        a_s = part_stats(q, ak, anchor_valid, score_scale)
        top = jnp.maximum(
            jnp.max(ws, axis=-1, keepdims=True), jnp.max(a_s, axis=-1, keepdims=True)
        )
        w_exp = jnp.exp(ws - top)
        a_exp = jnp.exp(a_s - top)
        total = jnp.sum(w_exp, axis=-1, keepdims=True) + jnp.sum(a_exp, axis=-1, keepdims=True)
        w_probs = (w_exp / total).astype(jnp.bfloat16)
        a_probs = (a_exp / total).astype(jnp.bfloat16)
        blended = jnp.einsum(
            "hqk,khd->hqd", w_probs, wv, preferred_element_type=jnp.float32
        ) + jnp.einsum("hqk,khd->hqd", a_probs, av, preferred_element_type=jnp.float32)
        pieces.append(jnp.transpose(blended, (1, 0, 2)).reshape(tok_rows, 4 * DH))
    attended = jnp.concatenate(pieces, axis=1)
    attended = jnp.where(row_ids[:, None] < lengths[place], attended, 0.0).astype(jnp.bfloat16)
    features = frames.astype(jnp.float32)
    squares = jnp.mean(features * features, axis=-1, keepdims=True)
    normed = features * lax.rsqrt(squares + 1e-06) * norm_gain
    activated = jax.nn.silu(normed).astype(jnp.bfloat16)
    stacked = jnp.concatenate([past_frames, activated], axis=0)
    extended = extended_2(stacked, (("span", 1),), 1)
    padded = jnp.pad(extended, ((0, 0), (0, 0), (1, 1), (0, 0)))
    frame_count = frames.shape[0]
    rows_here = frames.shape[1]
    col_count = frames.shape[2]
    channels = frames.shape[3]
    windows = []
    for frame_tap in range(3):
        for row_tap in range(3):
            for col_tap in range(3):
                windows.append(
                    padded[
                        frame_tap : frame_tap + frame_count,
                        row_tap : row_tap + rows_here,
                        col_tap : col_tap + col_count,
                        :,
                    ]
                )
    columns = jnp.concatenate(windows, axis=-1).reshape(-1, 27 * channels)
    convolved = jnp.dot(
        columns, conv_weight.reshape(27 * channels, channels), preferred_element_type=jnp.float32
    )
    decoded = features + conv_bias + convolved.reshape(frame_count, rows_here, col_count, channels)
    return (attended, decoded.astype(jnp.bfloat16))


def solution(mesh):
    placed = (
        P(("group", "span"), None),
        P(None, ("group", "span"), None),
        P("group"),
        P("group", None),
        P("group"),
        P("group", "span", None, None),
        P("group", "span", None, None),
        P(),
        P(),
        P(),
    )
    return jax.shard_map(
        shards,
        mesh=mesh,
        in_specs=placed,
        out_specs=(P(("group", "span"), None), P("group", "span", None, None)),
        check_vma=False,
    )
```

```python
import jax
import jax.numpy as jnp
from jax import lax
from jax.sharding import PartitionSpec as P

H = 20
DH = 128
WIN = 4
HG = 10


def spread(block, axis, source):
    block = jnp.where(lax.axis_index(axis) == source, block, jnp.zeros_like(block))
    return lax.psum(block, axis)


def extended_2(block, sides, width):
    for axis, dim in sides:
        count = lax.axis_size(axis)
        forward = [(i, i + 1) for i in range(count - 1)]
        backward = [(target, source) for source, target in forward]
        low = lax.ppermute(
            lax.slice_in_dim(block, block.shape[dim] - width, None, axis=dim), axis, forward
        )
        high = lax.ppermute(lax.slice_in_dim(block, 0, width, axis=dim), axis, backward)
        block = jnp.concatenate([low, block, high], axis=dim)
    return block


def move(value, pairs):
    return lax.ppermute(value, "span", pairs)


def window_blocks(kv, devices):
    rows = devices // 4
    lane = lax.axis_index("span") % 4

    def at(r, l):
        return 4 * (r % rows) + l

    rng = range(rows)
    rail1 = move(kv, [(at(r, 3), at(r + 1, 2)) for r in rng])
    rail0 = move(kv, [(at(r, 1), at(r + 1, 0)) for r in rng])
    y_up = move(kv, [(at(r, 0), at(r, 2)) for r in rng] + [(at(r, 1), at(r, 3)) for r in rng])
    y_down = move(kv, [(at(r, 2), at(r, 1)) for r in rng])
    chip = move(kv, [(at(r, 0), at(r, 1)) for r in rng] + [(at(r, 2), at(r, 3)) for r in rng])
    swap = move(y_up, [(at(r, 3), at(r, 2)) for r in rng] + [(at(r, 2), at(r, 3)) for r in rng])
    down2 = move(rail1, [(at(r, 2), at(r, 0)) for r in rng])
    rail0b = move(y_down, [(at(r, 1), at(r + 1, 0)) for r in rng])
    pair = move(jnp.stack([down2, rail0b]), [(at(r, 0), at(r, 1)) for r in rng])

    def pick(*options):
        out = options[0]
        for l in range(1, 4):
            out = jnp.where(lane == l, options[l], out)
        return out

    b1 = pick(down2, chip, swap, chip)
    b2 = pick(rail0b, pair[0], y_up, y_up)
    b3 = pick(rail0, pair[1], rail1, swap)
    return b1, b2, b3


def part_stats(q, k, valid, scale):
    scores = jnp.einsum("qhd,khd->hqk", q, k, preferred_element_type=jnp.float32) * scale
    return jnp.where(valid[None, None, :], scores, -jnp.inf)


def shards(
    queries,
    keys_values,
    owner,
    span_mask,
    lengths,
    frames,
    past_frames,
    norm_gain,
    conv_weight,
    conv_bias,
):
    devices = lax.axis_size("span")
    place = lax.axis_index("span")
    anchor = owner[0]
    position = (place - anchor - 1) % devices
    tok_rows = queries.shape[0]
    row_ids = jnp.arange(tok_rows, dtype=jnp.int32)
    anchor_k = spread(keys_values[0], "span", anchor)
    later_v, anchor_k = lax.optimization_barrier((keys_values[1], anchor_k))
    anchor_v = spread(later_v, "span", anchor)
    b1, b2, b3 = window_blocks(keys_values, devices)
    blocks = [keys_values, b1, b2, b3]
    valid_list = [row_ids < lengths[place]]
    for offset in range(1, WIN):
        source = (place - offset) % devices
        allowed = (position >= offset) & (span_mask[position, offset - 1] == 1)
        valid_list.append(allowed & (row_ids < lengths[source]))
    anchor_valid = (place != anchor) & (row_ids < lengths[anchor])
    window_kv = jnp.concatenate(blocks, axis=1)
    window_valid = jnp.concatenate(valid_list)
    score_scale = DH ** (-0.5)
    partial = []
    for head_block in range(H // HG):
        first_col = head_block * HG * DH
        last_col = first_col + HG * DH
        q = queries[:, first_col:last_col].reshape(tok_rows, HG, DH)
        wk = window_kv[0, :, first_col:last_col].reshape(-1, HG, DH)
        wv = window_kv[1, :, first_col:last_col].reshape(-1, HG, DH)
        ak = anchor_k[:, first_col:last_col].reshape(-1, HG, DH)
        ws = part_stats(q, wk, window_valid, score_scale)
        a_s = part_stats(q, ak, anchor_valid, score_scale)
        top = jnp.maximum(
            jnp.max(ws, axis=-1, keepdims=True), jnp.max(a_s, axis=-1, keepdims=True)
        )
        w_exp = jnp.exp(ws - top)
        a_exp = jnp.exp(a_s - top)
        total = jnp.sum(w_exp, axis=-1, keepdims=True) + jnp.sum(a_exp, axis=-1, keepdims=True)
        w_probs = (w_exp / total).astype(jnp.bfloat16)
        a_probs = (a_exp / total).astype(jnp.bfloat16)
        w_out = jnp.einsum("hqk,khd->hqd", w_probs, wv, preferred_element_type=jnp.float32)
        partial.append((w_out, a_probs))
    anchor_v, partial = lax.optimization_barrier((anchor_v, partial))
    pieces = []
    for head_block, (w_out, a_probs) in enumerate(partial):
        first_col = head_block * HG * DH
        last_col = first_col + HG * DH
        av = anchor_v[:, first_col:last_col].reshape(-1, HG, DH)
        blended = w_out + jnp.einsum(
            "hqk,khd->hqd", a_probs, av, preferred_element_type=jnp.float32
        )
        pieces.append(jnp.transpose(blended, (1, 0, 2)).reshape(tok_rows, HG * DH))
    attended = jnp.concatenate(pieces, axis=1)
    attended = jnp.where(row_ids[:, None] < lengths[place], attended, 0.0).astype(jnp.bfloat16)
    features = frames.astype(jnp.float32)
    squares = jnp.mean(features * features, axis=-1, keepdims=True)
    normed = features * lax.rsqrt(squares + 1e-06) * norm_gain
    activated = jax.nn.silu(normed).astype(jnp.bfloat16)
    stacked = jnp.concatenate([past_frames, activated], axis=0)
    extended = extended_2(stacked, (("span", 1),), 1)
    padded = jnp.pad(extended, ((0, 0), (0, 0), (1, 1), (0, 0)))
    frame_count = frames.shape[0]
    rows_here = frames.shape[1]
    col_count = frames.shape[2]
    channels = frames.shape[3]
    windows = []
    for frame_tap in range(3):
        for row_tap in range(3):
            for col_tap in range(3):
                windows.append(
                    padded[
                        frame_tap : frame_tap + frame_count,
                        row_tap : row_tap + rows_here,
                        col_tap : col_tap + col_count,
                        :,
                    ]
                )
    columns = jnp.concatenate(windows, axis=-1).reshape(-1, 27 * channels)
    convolved = jnp.dot(
        columns, conv_weight.reshape(27 * channels, channels), preferred_element_type=jnp.float32
    )
    decoded = features + conv_bias + convolved.reshape(frame_count, rows_here, col_count, channels)
    return (attended, decoded.astype(jnp.bfloat16))


def solution(mesh):
    placed = (
        P(("group", "span"), None),
        P(None, ("group", "span"), None),
        P("group"),
        P("group", None),
        P("group"),
        P("group", "span", None, None),
        P("group", "span", None, None),
        P(),
        P(),
        P(),
    )
    return jax.shard_map(
        shards,
        mesh=mesh,
        in_specs=placed,
        out_specs=(P(("group", "span"), None), P("group", "span", None, None)),
        check_vma=False,
    )
```

```python
import jax
import jax.numpy as jnp
from jax import lax
from jax.sharding import PartitionSpec as P

H = 20
DH = 128
WIN = 4
HG = 10


def spread(block, axis, source):
    block = jnp.where(lax.axis_index(axis) == source, block, jnp.zeros_like(block))
    return lax.psum(block, axis)


def extended_2(block, sides, width):
    for axis, dim in sides:
        count = lax.axis_size(axis)
        forward = [(i, i + 1) for i in range(count - 1)]
        backward = [(target, source) for source, target in forward]
        low = lax.ppermute(
            lax.slice_in_dim(block, block.shape[dim] - width, None, axis=dim), axis, forward
        )
        high = lax.ppermute(lax.slice_in_dim(block, 0, width, axis=dim), axis, backward)
        block = jnp.concatenate([low, block, high], axis=dim)
    return block


def move(value, pairs):
    return lax.ppermute(value, "span", pairs)


def window_blocks(kv, devices):
    rows = devices // 4
    lane = lax.axis_index("span") % 4

    def at(r, l):
        return 4 * (r % rows) + l

    rng = range(rows)
    rail1 = move(kv, [(at(r, 3), at(r + 1, 2)) for r in rng])
    rail0 = move(kv, [(at(r, 1), at(r + 1, 0)) for r in rng])
    y_up = move(kv, [(at(r, 0), at(r, 2)) for r in rng] + [(at(r, 1), at(r, 3)) for r in rng])
    y_down = move(kv, [(at(r, 2), at(r, 1)) for r in rng])
    chip = move(kv, [(at(r, 0), at(r, 1)) for r in rng] + [(at(r, 2), at(r, 3)) for r in rng])
    swap = move(y_up, [(at(r, 3), at(r, 2)) for r in rng] + [(at(r, 2), at(r, 3)) for r in rng])
    down2 = move(rail1, [(at(r, 2), at(r, 0)) for r in rng])
    rail0b = move(y_down, [(at(r, 1), at(r + 1, 0)) for r in rng])
    pair = move(jnp.stack([down2, rail0b]), [(at(r, 0), at(r, 1)) for r in rng])

    def pick(*options):
        out = options[0]
        for l in range(1, 4):
            out = jnp.where(lane == l, options[l], out)
        return out

    b1 = pick(down2, chip, swap, chip)
    b2 = pick(rail0b, pair[0], y_up, y_up)
    b3 = pick(rail0, pair[1], rail1, swap)
    return b1, b2, b3


def part_stats(q, k, valid, scale):
    scores = jnp.einsum("qhd,khd->hqk", q, k, preferred_element_type=jnp.float32) * scale
    return jnp.where(valid[None, None, :], scores, -jnp.inf)


def weighted(weights, values):
    return jnp.einsum(
        "hqk,khd->hqd", weights.astype(jnp.bfloat16), values, preferred_element_type=jnp.float32
    )


def shards(
    queries,
    keys_values,
    owner,
    span_mask,
    lengths,
    frames,
    past_frames,
    norm_gain,
    conv_weight,
    conv_bias,
):
    devices = lax.axis_size("span")
    place = lax.axis_index("span")
    anchor = owner[0]
    position = (place - anchor - 1) % devices
    tok_rows = queries.shape[0]
    row_ids = jnp.arange(tok_rows, dtype=jnp.int32)
    anchor_kv = spread(keys_values, "span", anchor)
    b1, b2, b3 = window_blocks(keys_values, devices)
    blocks = [keys_values, b1, b2, b3]
    valid_list = [row_ids < lengths[place]]
    for offset in range(1, WIN):
        source = (place - offset) % devices
        allowed = (position >= offset) & (span_mask[position, offset - 1] == 1)
        valid_list.append(allowed & (row_ids < lengths[source]))
    anchor_valid = (place != anchor) & (row_ids < lengths[anchor])
    window_kv = jnp.concatenate(blocks, axis=1)
    window_valid = jnp.concatenate(valid_list)
    score_scale = DH ** (-0.5)
    partial = []
    for head_block in range(H // HG):
        first_col = head_block * HG * DH
        last_col = first_col + HG * DH
        q = queries[:, first_col:last_col].reshape(tok_rows, HG, DH)
        wk = window_kv[0, :, first_col:last_col].reshape(-1, HG, DH)
        wv = window_kv[1, :, first_col:last_col].reshape(-1, HG, DH)
        ws = part_stats(q, wk, window_valid, score_scale)
        w_max = jnp.max(ws, axis=-1, keepdims=True)
        w_exp = jnp.exp(ws - w_max)
        w_sum = jnp.sum(w_exp, axis=-1, keepdims=True)
        partial.append((w_max, w_sum, weighted(w_exp, wv)))
    anchor_kv, partial = lax.optimization_barrier((anchor_kv, partial))
    pieces = []
    for head_block, (w_max, w_sum, w_out) in enumerate(partial):
        first_col = head_block * HG * DH
        last_col = first_col + HG * DH
        q = queries[:, first_col:last_col].reshape(tok_rows, HG, DH)
        ak = anchor_kv[0, :, first_col:last_col].reshape(-1, HG, DH)
        av = anchor_kv[1, :, first_col:last_col].reshape(-1, HG, DH)
        a_s = part_stats(q, ak, anchor_valid, score_scale)
        top = jnp.maximum(w_max, jnp.max(a_s, axis=-1, keepdims=True))
        a_exp = jnp.exp(a_s - top)
        a_sum = jnp.sum(a_exp, axis=-1, keepdims=True)
        a_out = weighted(a_exp, av)
        w_scale = jnp.exp(w_max - top)
        blended = (w_out * w_scale + a_out) / (w_sum * w_scale + a_sum)
        pieces.append(jnp.transpose(blended, (1, 0, 2)).reshape(tok_rows, HG * DH))
    attended = jnp.concatenate(pieces, axis=1)
    attended = jnp.where(row_ids[:, None] < lengths[place], attended, 0.0).astype(jnp.bfloat16)
    features = frames.astype(jnp.float32)
    squares = jnp.mean(features * features, axis=-1, keepdims=True)
    normed = features * lax.rsqrt(squares + 1e-06) * norm_gain
    activated = jax.nn.silu(normed).astype(jnp.bfloat16)
    stacked = jnp.concatenate([past_frames, activated], axis=0)
    extended = extended_2(stacked, (("span", 1),), 1)
    padded = jnp.pad(extended, ((0, 0), (0, 0), (1, 1), (0, 0)))
    frame_count = frames.shape[0]
    rows_here = frames.shape[1]
    col_count = frames.shape[2]
    channels = frames.shape[3]
    windows = []
    for frame_tap in range(3):
        for row_tap in range(3):
            for col_tap in range(3):
                windows.append(
                    padded[
                        frame_tap : frame_tap + frame_count,
                        row_tap : row_tap + rows_here,
                        col_tap : col_tap + col_count,
                        :,
                    ]
                )
    columns = jnp.concatenate(windows, axis=-1).reshape(-1, 27 * channels)
    convolved = jnp.dot(
        columns, conv_weight.reshape(27 * channels, channels), preferred_element_type=jnp.float32
    )
    decoded = features + conv_bias + convolved.reshape(frame_count, rows_here, col_count, channels)
    return (attended, decoded.astype(jnp.bfloat16))


def solution(mesh):
    placed = (
        P(("group", "span"), None),
        P(None, ("group", "span"), None),
        P("group"),
        P("group", None),
        P("group"),
        P("group", "span", None, None),
        P("group", "span", None, None),
        P(),
        P(),
        P(),
    )
    return jax.shard_map(
        shards,
        mesh=mesh,
        in_specs=placed,
        out_specs=(P(("group", "span"), None), P("group", "span", None, None)),
        check_vma=False,
    )
```

```python
import jax
import jax.numpy as jnp
from jax import lax
from jax.sharding import PartitionSpec as P

H = 20
DH = 128
WIN = 4
HG = 10


def spread(block, axis, source):
    block = jnp.where(lax.axis_index(axis) == source, block, jnp.zeros_like(block))
    return lax.psum(block, axis)


def extended_2(block, sides, width):
    for axis, dim in sides:
        count = lax.axis_size(axis)
        forward = [(i, i + 1) for i in range(count - 1)]
        backward = [(target, source) for source, target in forward]
        low = lax.ppermute(
            lax.slice_in_dim(block, block.shape[dim] - width, None, axis=dim), axis, forward
        )
        high = lax.ppermute(lax.slice_in_dim(block, 0, width, axis=dim), axis, backward)
        block = jnp.concatenate([low, block, high], axis=dim)
    return block


def move(value, pairs):
    return lax.ppermute(value, "span", pairs)


def window_blocks(kv, devices):
    rows = devices // 4
    lane = lax.axis_index("span") % 4

    def at(r, l):
        return 4 * (r % rows) + l

    rng = range(rows)
    rail1 = move(kv, [(at(r, 3), at(r + 1, 2)) for r in rng])
    rail0 = move(kv, [(at(r, 1), at(r + 1, 0)) for r in rng])
    y_up = move(kv, [(at(r, 0), at(r, 2)) for r in rng] + [(at(r, 1), at(r, 3)) for r in rng])
    y_down = move(kv, [(at(r, 2), at(r, 1)) for r in rng])
    chip = move(kv, [(at(r, 0), at(r, 1)) for r in rng] + [(at(r, 2), at(r, 3)) for r in rng])
    swap = move(y_up, [(at(r, 3), at(r, 2)) for r in rng] + [(at(r, 2), at(r, 3)) for r in rng])
    down2 = move(rail1, [(at(r, 2), at(r, 0)) for r in rng])
    rail0b = move(y_down, [(at(r, 1), at(r + 1, 0)) for r in rng])
    pair = move(jnp.stack([down2, rail0b]), [(at(r, 0), at(r, 1)) for r in rng])

    def pick(*options):
        out = options[0]
        for l in range(1, 4):
            out = jnp.where(lane == l, options[l], out)
        return out

    b1 = pick(down2, chip, swap, chip)
    b2 = pick(rail0b, pair[0], y_up, y_up)
    b3 = pick(rail0, pair[1], rail1, swap)
    return b1, b2, b3


def part_stats(q, k, valid, scale):
    scores = jnp.einsum("qhd,khd->hqk", q, k, preferred_element_type=jnp.float32) * scale
    return jnp.where(valid[None, None, :], scores, -jnp.inf)


def weighted(weights, values):
    return jnp.einsum(
        "hqk,khd->hqd", weights.astype(jnp.bfloat16), values, preferred_element_type=jnp.float32
    )


def shards(
    queries,
    keys_values,
    owner,
    span_mask,
    lengths,
    frames,
    past_frames,
    norm_gain,
    conv_weight,
    conv_bias,
):
    devices = lax.axis_size("span")
    place = lax.axis_index("span")
    anchor = owner[0]
    position = (place - anchor - 1) % devices
    tok_rows = queries.shape[0]
    row_ids = jnp.arange(tok_rows, dtype=jnp.int32)
    is_anchor = place == anchor
    masked = jnp.where(is_anchor, keys_values, jnp.zeros_like(keys_values))
    anchor_kv = lax.psum(masked, "span")
    sent = jnp.where(is_anchor, lax.optimization_barrier(masked), keys_values)
    b1, b2, b3 = window_blocks(sent, devices)
    blocks = [keys_values, b1, b2, b3]
    valid_list = [row_ids < lengths[place]]
    for offset in range(1, WIN):
        source = (place - offset) % devices
        allowed = (position >= offset) & (span_mask[position, offset - 1] == 1)
        valid_list.append(allowed & (row_ids < lengths[source]))
    anchor_valid = (place != anchor) & (row_ids < lengths[anchor])
    window_kv = jnp.concatenate(blocks, axis=1)
    window_valid = jnp.concatenate(valid_list)
    score_scale = DH ** (-0.5)
    partial = []
    for head_block in range(H // HG):
        first_col = head_block * HG * DH
        last_col = first_col + HG * DH
        q = queries[:, first_col:last_col].reshape(tok_rows, HG, DH)
        wk = window_kv[0, :, first_col:last_col].reshape(-1, HG, DH)
        wv = window_kv[1, :, first_col:last_col].reshape(-1, HG, DH)
        ws = part_stats(q, wk, window_valid, score_scale)
        w_max = jnp.max(ws, axis=-1, keepdims=True)
        w_exp = jnp.exp(ws - w_max)
        w_sum = jnp.sum(w_exp, axis=-1, keepdims=True)
        partial.append((w_max, w_sum, weighted(w_exp, wv)))
    anchor_kv, partial = lax.optimization_barrier((anchor_kv, partial))
    pieces = []
    for head_block, (w_max, w_sum, w_out) in enumerate(partial):
        first_col = head_block * HG * DH
        last_col = first_col + HG * DH
        q = queries[:, first_col:last_col].reshape(tok_rows, HG, DH)
        ak = anchor_kv[0, :, first_col:last_col].reshape(-1, HG, DH)
        av = anchor_kv[1, :, first_col:last_col].reshape(-1, HG, DH)
        a_s = part_stats(q, ak, anchor_valid, score_scale)
        top = jnp.maximum(w_max, jnp.max(a_s, axis=-1, keepdims=True))
        a_exp = jnp.exp(a_s - top)
        a_sum = jnp.sum(a_exp, axis=-1, keepdims=True)
        a_out = weighted(a_exp, av)
        w_scale = jnp.exp(w_max - top)
        blended = (w_out * w_scale + a_out) / (w_sum * w_scale + a_sum)
        pieces.append(jnp.transpose(blended, (1, 0, 2)).reshape(tok_rows, HG * DH))
    attended = jnp.concatenate(pieces, axis=1)
    attended = jnp.where(row_ids[:, None] < lengths[place], attended, 0.0).astype(jnp.bfloat16)
    features = frames.astype(jnp.float32)
    squares = jnp.mean(features * features, axis=-1, keepdims=True)
    normed = features * lax.rsqrt(squares + 1e-06) * norm_gain
    activated = jax.nn.silu(normed).astype(jnp.bfloat16)
    stacked = jnp.concatenate([past_frames, activated], axis=0)
    extended = extended_2(stacked, (("span", 1),), 1)
    padded = jnp.pad(extended, ((0, 0), (0, 0), (1, 1), (0, 0)))
    frame_count = frames.shape[0]
    rows_here = frames.shape[1]
    col_count = frames.shape[2]
    channels = frames.shape[3]
    windows = []
    for frame_tap in range(3):
        for row_tap in range(3):
            for col_tap in range(3):
                windows.append(
                    padded[
                        frame_tap : frame_tap + frame_count,
                        row_tap : row_tap + rows_here,
                        col_tap : col_tap + col_count,
                        :,
                    ]
                )
    columns = jnp.concatenate(windows, axis=-1).reshape(-1, 27 * channels)
    convolved = jnp.dot(
        columns, conv_weight.reshape(27 * channels, channels), preferred_element_type=jnp.float32
    )
    decoded = features + conv_bias + convolved.reshape(frame_count, rows_here, col_count, channels)
    return (attended, decoded.astype(jnp.bfloat16))


def solution(mesh):
    placed = (
        P(("group", "span"), None),
        P(None, ("group", "span"), None),
        P("group"),
        P("group", None),
        P("group"),
        P("group", "span", None, None),
        P("group", "span", None, None),
        P(),
        P(),
        P(),
    )
    return jax.shard_map(
        shards,
        mesh=mesh,
        in_specs=placed,
        out_specs=(P(("group", "span"), None), P("group", "span", None, None)),
        check_vma=False,
    )
```

```python
import jax
import jax.numpy as jnp
from jax import lax
from jax.sharding import PartitionSpec as P

H = 20
DH = 128
WIN = 4
HG = 10


def spread(block, axis, source):
    block = jnp.where(lax.axis_index(axis) == source, block, jnp.zeros_like(block))
    return lax.psum(block, axis)


def extended_2(block, sides, width):
    for axis, dim in sides:
        count = lax.axis_size(axis)
        forward = [(i, i + 1) for i in range(count - 1)]
        backward = [(target, source) for source, target in forward]
        low = lax.ppermute(
            lax.slice_in_dim(block, block.shape[dim] - width, None, axis=dim), axis, forward
        )
        high = lax.ppermute(lax.slice_in_dim(block, 0, width, axis=dim), axis, backward)
        block = jnp.concatenate([low, block, high], axis=dim)
    return block


def move(value, pairs):
    return lax.ppermute(value, "span", pairs)


def window_blocks(kv, devices):
    rows = devices // 4
    lane = lax.axis_index("span") % 4

    def at(r, l):
        return 4 * (r % rows) + l

    def pairs(*moves):
        return [(at(r, a), at(r + step, b)) for a, b, step in moves for r in range(rows)]

    def pick(*options):
        out = options[0]
        for l in range(1, 4):
            out = jnp.where(lane == l, options[l], out)
        return out

    cross = move(kv, pairs((0, 2, 0), (1, 3, 0), (2, 1, 0)))
    along = move(kv, pairs((0, 1, 0), (2, 3, 0), (1, 0, 1), (3, 2, 1)))
    second = move(pick(cross, cross, along, cross), pairs((3, 2, 0), (2, 0, 0), (1, 1, 1)))
    third = move(pick(second, second, cross, cross), pairs((0, 1, 0), (1, 0, 0), (2, 3, 0)))
    b1 = pick(second, along, second, along)
    b2 = pick(third, third, cross, cross)
    b3 = pick(along, second, along, third)
    return b1, b2, b3


def part_stats(q, k, valid, scale):
    scores = jnp.einsum("qhd,khd->hqk", q, k, preferred_element_type=jnp.float32) * scale
    return jnp.where(valid[None, None, :], scores, -jnp.inf)


def weighted(weights, values):
    return jnp.einsum(
        "hqk,khd->hqd", weights.astype(jnp.bfloat16), values, preferred_element_type=jnp.float32
    )


def shards(
    queries,
    keys_values,
    owner,
    span_mask,
    lengths,
    frames,
    past_frames,
    norm_gain,
    conv_weight,
    conv_bias,
):
    devices = lax.axis_size("span")
    place = lax.axis_index("span")
    anchor = owner[0]
    position = (place - anchor - 1) % devices
    tok_rows = queries.shape[0]
    row_ids = jnp.arange(tok_rows, dtype=jnp.int32)
    is_anchor = place == anchor
    masked = jnp.where(is_anchor, keys_values, jnp.zeros_like(keys_values))
    anchor_kv = lax.psum(masked, "span")
    sent = jnp.where(is_anchor, lax.optimization_barrier(masked), keys_values)
    b1, b2, b3 = window_blocks(sent, devices)
    blocks = [keys_values, b1, b2, b3]
    valid_list = [row_ids < lengths[place]]
    for offset in range(1, WIN):
        source = (place - offset) % devices
        allowed = (position >= offset) & (span_mask[position, offset - 1] == 1)
        valid_list.append(allowed & (row_ids < lengths[source]))
    anchor_valid = (place != anchor) & (row_ids < lengths[anchor])
    window_kv = jnp.concatenate(blocks, axis=1)
    window_valid = jnp.concatenate(valid_list)
    score_scale = DH ** (-0.5)
    partial = []
    for head_block in range(H // HG):
        first_col = head_block * HG * DH
        last_col = first_col + HG * DH
        q = queries[:, first_col:last_col].reshape(tok_rows, HG, DH)
        wk = window_kv[0, :, first_col:last_col].reshape(-1, HG, DH)
        wv = window_kv[1, :, first_col:last_col].reshape(-1, HG, DH)
        ws = part_stats(q, wk, window_valid, score_scale)
        w_max = jnp.max(ws, axis=-1, keepdims=True)
        w_exp = jnp.exp(ws - w_max)
        w_sum = jnp.sum(w_exp, axis=-1, keepdims=True)
        partial.append((w_max, w_sum, weighted(w_exp, wv)))
    anchor_kv, partial = lax.optimization_barrier((anchor_kv, partial))
    pieces = []
    for head_block, (w_max, w_sum, w_out) in enumerate(partial):
        first_col = head_block * HG * DH
        last_col = first_col + HG * DH
        q = queries[:, first_col:last_col].reshape(tok_rows, HG, DH)
        ak = anchor_kv[0, :, first_col:last_col].reshape(-1, HG, DH)
        av = anchor_kv[1, :, first_col:last_col].reshape(-1, HG, DH)
        a_s = part_stats(q, ak, anchor_valid, score_scale)
        top = jnp.maximum(w_max, jnp.max(a_s, axis=-1, keepdims=True))
        a_exp = jnp.exp(a_s - top)
        a_sum = jnp.sum(a_exp, axis=-1, keepdims=True)
        a_out = weighted(a_exp, av)
        w_scale = jnp.exp(w_max - top)
        blended = (w_out * w_scale + a_out) / (w_sum * w_scale + a_sum)
        pieces.append(jnp.transpose(blended, (1, 0, 2)).reshape(tok_rows, HG * DH))
    attended = jnp.concatenate(pieces, axis=1)
    attended = jnp.where(row_ids[:, None] < lengths[place], attended, 0.0).astype(jnp.bfloat16)
    features = frames.astype(jnp.float32)
    squares = jnp.mean(features * features, axis=-1, keepdims=True)
    normed = features * lax.rsqrt(squares + 1e-06) * norm_gain
    activated = jax.nn.silu(normed).astype(jnp.bfloat16)
    stacked = jnp.concatenate([past_frames, activated], axis=0)
    extended = extended_2(stacked, (("span", 1),), 1)
    padded = jnp.pad(extended, ((0, 0), (0, 0), (1, 1), (0, 0)))
    frame_count = frames.shape[0]
    rows_here = frames.shape[1]
    col_count = frames.shape[2]
    channels = frames.shape[3]
    windows = []
    for frame_tap in range(3):
        for row_tap in range(3):
            for col_tap in range(3):
                windows.append(
                    padded[
                        frame_tap : frame_tap + frame_count,
                        row_tap : row_tap + rows_here,
                        col_tap : col_tap + col_count,
                        :,
                    ]
                )
    columns = jnp.concatenate(windows, axis=-1).reshape(-1, 27 * channels)
    convolved = jnp.dot(
        columns, conv_weight.reshape(27 * channels, channels), preferred_element_type=jnp.float32
    )
    decoded = features + conv_bias + convolved.reshape(frame_count, rows_here, col_count, channels)
    return (attended, decoded.astype(jnp.bfloat16))


def solution(mesh):
    placed = (
        P(("group", "span"), None),
        P(None, ("group", "span"), None),
        P("group"),
        P("group", None),
        P("group"),
        P("group", "span", None, None),
        P("group", "span", None, None),
        P(),
        P(),
        P(),
    )
    return jax.shard_map(
        shards,
        mesh=mesh,
        in_specs=placed,
        out_specs=(P(("group", "span"), None), P("group", "span", None, None)),
        check_vma=False,
    )
```

```python
import jax
import jax.numpy as jnp
from jax import lax
from jax.sharding import PartitionSpec as P

H = 20
DH = 128
WIN = 4
HG = 20


def spread(block, axis, source):
    block = jnp.where(lax.axis_index(axis) == source, block, jnp.zeros_like(block))
    return lax.psum(block, axis)


def extended_2(block, sides, width):
    for axis, dim in sides:
        count = lax.axis_size(axis)
        forward = [(i, i + 1) for i in range(count - 1)]
        backward = [(target, source) for source, target in forward]
        low = lax.ppermute(
            lax.slice_in_dim(block, block.shape[dim] - width, None, axis=dim), axis, forward
        )
        high = lax.ppermute(lax.slice_in_dim(block, 0, width, axis=dim), axis, backward)
        block = jnp.concatenate([low, block, high], axis=dim)
    return block


def move(value, pairs):
    return lax.ppermute(value, "span", pairs)


def window_blocks(kv, devices, after, after_second):
    rows = devices // 4
    lane = lax.axis_index("span") % 4

    def at(r, l):
        return 4 * (r % rows) + l

    def pairs(*moves):
        return [(at(r, a), at(r + step, b)) for a, b, step in moves for r in range(rows)]

    def pick(*options):
        out = options[0]
        for l in range(1, 4):
            out = jnp.where(lane == l, options[l], out)
        return out

    cross = move(kv, pairs((0, 2, 0), (1, 3, 0), (2, 1, 0)))
    along = move(kv, pairs((0, 1, 0), (2, 3, 0), (1, 0, 1), (3, 2, 1)))
    second = move(pick(cross, cross, along, cross), pairs((3, 2, 0), (2, 0, 0), (1, 1, 1)))
    carry = after(along, cross)
    payload, carry = lax.optimization_barrier((pick(second, second, cross, cross), carry))
    third = move(payload, pairs((0, 1, 0), (1, 0, 0), (2, 3, 0)))
    carry = after_second(carry, cross, second)
    return third, carry


def part_stats(q, k, valid, scale):
    scores = jnp.einsum("qhd,khd->hqk", q, k, preferred_element_type=jnp.float32) * scale
    return jnp.where(valid[None, None, :], scores, -jnp.inf)


def weighted(weights, values):
    return jnp.einsum(
        "hqk,khd->hqd", weights.astype(jnp.bfloat16), values, preferred_element_type=jnp.float32
    )


def attend(q, kv, valid, state):
    k = kv[0].reshape(-1, HG, DH)
    v = kv[1].reshape(-1, HG, DH)
    scores = part_stats(q, k, valid, DH ** (-0.5))
    top = jnp.max(scores, axis=-1, keepdims=True)
    if state is not None:
        top = jnp.maximum(state[0], top)
    weights = jnp.exp(scores - top)
    total = jnp.sum(weights, axis=-1, keepdims=True)
    out = weighted(weights, v)
    if state is not None:
        rescale = jnp.exp(state[0] - top)
        total = state[1] * rescale + total
        out = state[2] * rescale + out
    return top, total, out


def shards(
    queries,
    keys_values,
    owner,
    span_mask,
    lengths,
    frames,
    past_frames,
    norm_gain,
    conv_weight,
    conv_bias,
):
    devices = lax.axis_size("span")
    place = lax.axis_index("span")
    anchor = owner[0]
    position = (place - anchor - 1) % devices
    tok_rows = queries.shape[0]
    row_ids = jnp.arange(tok_rows, dtype=jnp.int32)
    is_anchor = place == anchor
    masked = jnp.where(is_anchor, keys_values, jnp.zeros_like(keys_values))
    anchor_kv = lax.psum(masked, "span")
    sent = jnp.where(is_anchor, lax.optimization_barrier(masked), keys_values)
    valid_list = [row_ids < lengths[place]]
    for offset in range(1, WIN):
        source = (place - offset) % devices
        allowed = (position >= offset) & (span_mask[position, offset - 1] == 1)
        valid_list.append(allowed & (row_ids < lengths[source]))
    valid_list.append(jnp.zeros_like(valid_list[0]))
    lane = place % 4

    def offset_of(*per_lane):
        out = valid_list[per_lane[0]]
        for l in range(1, 4):
            out = jnp.where(lane == l, valid_list[per_lane[l]], out)
        return out

    query_heads = queries.reshape(tok_rows, HG, DH)

    def first_group(along, cross):
        group_kv = jnp.concatenate([keys_values, along], axis=1)
        group_valid = jnp.concatenate([valid_list[0], offset_of(3, 1, 3, 1)])
        return attend(query_heads, group_kv, group_valid, None)

    def second_group(state, cross, second):
        group_kv = jnp.concatenate([cross, second], axis=1)
        group_valid = jnp.concatenate([offset_of(4, 4, 2, 2), offset_of(1, 3, 1, 4)])
        return attend(query_heads, group_kv, group_valid, state)

    third, state = window_blocks(sent, devices, first_group, second_group)
    state = attend(query_heads, third, offset_of(2, 2, 4, 3), state)
    anchor_valid = (place != anchor) & (row_ids < lengths[anchor])
    anchor_kv, state = lax.optimization_barrier((anchor_kv, state))
    top, total, out = attend(query_heads, anchor_kv, anchor_valid, state)
    blended = out / total
    pieces = [jnp.transpose(blended, (1, 0, 2)).reshape(tok_rows, HG * DH)]
    attended = jnp.concatenate(pieces, axis=1)
    attended = jnp.where(row_ids[:, None] < lengths[place], attended, 0.0).astype(jnp.bfloat16)
    features = frames.astype(jnp.float32)
    squares = jnp.mean(features * features, axis=-1, keepdims=True)
    normed = features * lax.rsqrt(squares + 1e-06) * norm_gain
    activated = jax.nn.silu(normed).astype(jnp.bfloat16)
    stacked = jnp.concatenate([past_frames, activated], axis=0)
    extended = extended_2(stacked, (("span", 1),), 1)
    padded = jnp.pad(extended, ((0, 0), (0, 0), (1, 1), (0, 0)))
    frame_count = frames.shape[0]
    rows_here = frames.shape[1]
    col_count = frames.shape[2]
    channels = frames.shape[3]
    windows = []
    for frame_tap in range(3):
        for row_tap in range(3):
            for col_tap in range(3):
                windows.append(
                    padded[
                        frame_tap : frame_tap + frame_count,
                        row_tap : row_tap + rows_here,
                        col_tap : col_tap + col_count,
                        :,
                    ]
                )
    columns = jnp.concatenate(windows, axis=-1).reshape(-1, 27 * channels)
    convolved = jnp.dot(
        columns, conv_weight.reshape(27 * channels, channels), preferred_element_type=jnp.float32
    )
    decoded = features + conv_bias + convolved.reshape(frame_count, rows_here, col_count, channels)
    return (attended, decoded.astype(jnp.bfloat16))


def solution(mesh):
    placed = (
        P(("group", "span"), None),
        P(None, ("group", "span"), None),
        P("group"),
        P("group", None),
        P("group"),
        P("group", "span", None, None),
        P("group", "span", None, None),
        P(),
        P(),
        P(),
    )
    return jax.shard_map(
        shards,
        mesh=mesh,
        in_specs=placed,
        out_specs=(P(("group", "span"), None), P("group", "span", None, None)),
        check_vma=False,
    )
```

```python
import jax
import jax.numpy as jnp
from jax import lax
from jax.sharding import PartitionSpec as P

H = 20
DH = 128
WIN = 4
HG = 10


def spread(block, axis, source):
    block = jnp.where(lax.axis_index(axis) == source, block, jnp.zeros_like(block))
    return lax.psum(block, axis)


def extended_2(block, sides, width):
    for axis, dim in sides:
        count = lax.axis_size(axis)
        forward = [(i, i + 1) for i in range(count - 1)]
        backward = [(target, source) for source, target in forward]
        low = lax.ppermute(
            lax.slice_in_dim(block, block.shape[dim] - width, None, axis=dim), axis, forward
        )
        high = lax.ppermute(lax.slice_in_dim(block, 0, width, axis=dim), axis, backward)
        block = jnp.concatenate([low, block, high], axis=dim)
    return block


def move(value, pairs):
    return lax.ppermute(value, "span", pairs)


def window_blocks(kv, devices):
    rows = devices // 4
    lane = lax.axis_index("span") % 4

    def at(r, l):
        return 4 * (r % rows) + l

    def pairs(*moves):
        return [(at(r, a), at(r + step, b)) for a, b, step in moves for r in range(rows)]

    def pick(*options):
        out = options[0]
        for l in range(1, 4):
            out = jnp.where(lane == l, options[l], out)
        return out

    cross = move(kv, pairs((0, 2, 0), (1, 3, 0), (2, 1, 0)))
    along = move(kv, pairs((0, 1, 0), (2, 3, 0), (1, 0, 1), (3, 2, 1)))
    second = move(pick(cross, cross, along, cross), pairs((3, 2, 0), (2, 0, 0), (1, 1, 1)))
    third = move(pick(second, second, cross, cross), pairs((0, 1, 0), (1, 0, 0), (2, 3, 0)))
    return along, cross, second, third


def part_stats(q, k, valid, scale):
    scores = jnp.einsum("qhd,khd->hqk", q, k, preferred_element_type=jnp.float32) * scale
    return jnp.where(valid[None, None, :], scores, -jnp.inf)


def weighted(weights, values):
    return jnp.einsum(
        "hqk,khd->hqd", weights.astype(jnp.bfloat16), values, preferred_element_type=jnp.float32
    )


def attend(q, kv, valid, state):
    k = kv[0].reshape(-1, HG, DH)
    v = kv[1].reshape(-1, HG, DH)
    scores = part_stats(q, k, valid, DH ** (-0.5))
    top = jnp.max(scores, axis=-1, keepdims=True)
    if state is not None:
        top = jnp.maximum(state[0], top)
    weights = jnp.exp(scores - top)
    total = jnp.sum(weights, axis=-1, keepdims=True)
    out = weighted(weights, v)
    if state is not None:
        rescale = jnp.exp(state[0] - top)
        total = state[1] * rescale + total
        out = state[2] * rescale + out
    return top, total, out


def shards(
    queries,
    keys_values,
    owner,
    span_mask,
    lengths,
    frames,
    past_frames,
    norm_gain,
    conv_weight,
    conv_bias,
):
    devices = lax.axis_size("span")
    place = lax.axis_index("span")
    anchor = owner[0]
    position = (place - anchor - 1) % devices
    tok_rows = queries.shape[0]
    row_ids = jnp.arange(tok_rows, dtype=jnp.int32)
    is_anchor = place == anchor
    masked = jnp.where(is_anchor, keys_values, jnp.zeros_like(keys_values))
    anchor_kv = lax.psum(masked, "span")
    sent = jnp.where(is_anchor, lax.optimization_barrier(masked), keys_values)
    along, cross, second, third = window_blocks(sent, devices)
    valid_list = [row_ids < lengths[place]]
    for offset in range(1, WIN):
        source = (place - offset) % devices
        allowed = (position >= offset) & (span_mask[position, offset - 1] == 1)
        valid_list.append(allowed & (row_ids < lengths[source]))
    valid_list.append(jnp.zeros_like(valid_list[0]))
    lane = place % 4

    def offset_of(*per_lane):
        out = valid_list[per_lane[0]]
        for l in range(1, 4):
            out = jnp.where(lane == l, valid_list[per_lane[l]], out)
        return out

    groups = [
        (jnp.concatenate([keys_values, along], axis=1),
         jnp.concatenate([valid_list[0], offset_of(3, 1, 3, 1)])),
        (jnp.concatenate([cross, second, third], axis=1),
         jnp.concatenate([offset_of(4, 4, 2, 2), offset_of(1, 3, 1, 4), offset_of(2, 2, 4, 3)])),
    ]
    anchor_valid = (place != anchor) & (row_ids < lengths[anchor])
    heads = [slice(h * HG * DH, (h + 1) * HG * DH) for h in range(H // HG)]
    query_heads = [queries[:, cols].reshape(tok_rows, HG, DH) for cols in heads]
    states = [None] * len(heads)
    for group_kv, group_valid in groups:
        for h, cols in enumerate(heads):
            states[h] = attend(query_heads[h], group_kv[:, :, cols], group_valid, states[h])
    anchor_kv, states = lax.optimization_barrier((anchor_kv, states))
    pieces = []
    for h, cols in enumerate(heads):
        top, total, out = attend(query_heads[h], anchor_kv[:, :, cols], anchor_valid, states[h])
        blended = out / total
        pieces.append(jnp.transpose(blended, (1, 0, 2)).reshape(tok_rows, HG * DH))
    attended = jnp.concatenate(pieces, axis=1)
    attended = jnp.where(row_ids[:, None] < lengths[place], attended, 0.0).astype(jnp.bfloat16)
    features = frames.astype(jnp.float32)
    squares = jnp.mean(features * features, axis=-1, keepdims=True)
    normed = features * lax.rsqrt(squares + 1e-06) * norm_gain
    activated = jax.nn.silu(normed).astype(jnp.bfloat16)
    stacked = jnp.concatenate([past_frames, activated], axis=0)
    extended = extended_2(stacked, (("span", 1),), 1)
    padded = jnp.pad(extended, ((0, 0), (0, 0), (1, 1), (0, 0)))
    frame_count = frames.shape[0]
    rows_here = frames.shape[1]
    col_count = frames.shape[2]
    channels = frames.shape[3]
    windows = []
    for frame_tap in range(3):
        for row_tap in range(3):
            for col_tap in range(3):
                windows.append(
                    padded[
                        frame_tap : frame_tap + frame_count,
                        row_tap : row_tap + rows_here,
                        col_tap : col_tap + col_count,
                        :,
                    ]
                )
    columns = jnp.concatenate(windows, axis=-1).reshape(-1, 27 * channels)
    convolved = jnp.dot(
        columns, conv_weight.reshape(27 * channels, channels), preferred_element_type=jnp.float32
    )
    decoded = features + conv_bias + convolved.reshape(frame_count, rows_here, col_count, channels)
    return (attended, decoded.astype(jnp.bfloat16))


def solution(mesh):
    placed = (
        P(("group", "span"), None),
        P(None, ("group", "span"), None),
        P("group"),
        P("group", None),
        P("group"),
        P("group", "span", None, None),
        P("group", "span", None, None),
        P(),
        P(),
        P(),
    )
    return jax.shard_map(
        shards,
        mesh=mesh,
        in_specs=placed,
        out_specs=(P(("group", "span"), None), P("group", "span", None, None)),
        check_vma=False,
    )
```

```python
import jax
import jax.numpy as jnp
from jax import lax
from jax.sharding import PartitionSpec as P

H = 20
DH = 128
WIN = 4
HG = 10


def spread(block, axis, source):
    block = jnp.where(lax.axis_index(axis) == source, block, jnp.zeros_like(block))
    return lax.psum(block, axis)


def extended_2(block, sides, width):
    for axis, dim in sides:
        count = lax.axis_size(axis)
        forward = [(i, i + 1) for i in range(count - 1)]
        backward = [(target, source) for source, target in forward]
        low = lax.ppermute(
            lax.slice_in_dim(block, block.shape[dim] - width, None, axis=dim), axis, forward
        )
        high = lax.ppermute(lax.slice_in_dim(block, 0, width, axis=dim), axis, backward)
        block = jnp.concatenate([low, block, high], axis=dim)
    return block


def move(value, pairs):
    return lax.ppermute(value, "span", pairs)


def window_blocks(kv, devices):
    rows = devices // 4
    lane = lax.axis_index("span") % 4

    def at(r, l):
        return 4 * (r % rows) + l

    def pairs(*moves):
        return [(at(r, a), at(r + step, b)) for a, b, step in moves for r in range(rows)]

    def pick(*options):
        out = options[0]
        for l in range(1, 4):
            out = jnp.where(lane == l, options[l], out)
        return out

    cross = move(kv, pairs((0, 2, 0), (1, 3, 0), (2, 1, 0)))
    along = move(kv, pairs((0, 1, 0), (2, 3, 0), (1, 0, 1), (3, 2, 1)))
    second = move(pick(cross, cross, along, cross), pairs((3, 2, 0), (2, 0, 0), (1, 1, 1)))
    third = move(pick(second, second, cross, cross), pairs((0, 1, 0), (1, 0, 0), (2, 3, 0)))
    return along, cross, second, third


def part_stats(q, k, valid, scale):
    scores = jnp.einsum("qhd,khd->hqk", q, k, preferred_element_type=jnp.float32) * scale
    return jnp.where(valid[None, None, :], scores, -jnp.inf)


def weighted(weights, values):
    return jnp.einsum(
        "hqk,khd->hqd", weights.astype(jnp.bfloat16), values, preferred_element_type=jnp.float32
    )


def attend(q, kv, valid, state):
    k = kv[0].reshape(-1, HG, DH)
    v = kv[1].reshape(-1, HG, DH)
    scores = part_stats(q, k, valid, DH ** (-0.5))
    top = jnp.max(scores, axis=-1, keepdims=True)
    if state is not None:
        top = jnp.maximum(state[0], top)
    weights = jnp.exp(scores - top)
    total = jnp.sum(weights, axis=-1, keepdims=True)
    out = weighted(weights, v)
    if state is not None:
        rescale = jnp.exp(state[0] - top)
        total = state[1] * rescale + total
        out = state[2] * rescale + out
    return top, total, out


def shards(
    queries,
    keys_values,
    owner,
    span_mask,
    lengths,
    frames,
    past_frames,
    norm_gain,
    conv_weight,
    conv_bias,
):
    devices = lax.axis_size("span")
    place = lax.axis_index("span")
    anchor = owner[0]
    position = (place - anchor - 1) % devices
    tok_rows = queries.shape[0]
    row_ids = jnp.arange(tok_rows, dtype=jnp.int32)
    is_anchor = place == anchor
    masked = jnp.where(is_anchor, keys_values, jnp.zeros_like(keys_values))
    anchor_kv = lax.psum(masked, "span")
    sent = jnp.where(is_anchor, lax.optimization_barrier(masked), keys_values)
    along, cross, second, third = window_blocks(sent, devices)
    valid_list = [row_ids < lengths[place]]
    for offset in range(1, WIN):
        source = (place - offset) % devices
        allowed = (position >= offset) & (span_mask[position, offset - 1] == 1)
        valid_list.append(allowed & (row_ids < lengths[source]))
    valid_list.append(jnp.zeros_like(valid_list[0]))
    lane = place % 4

    def offset_of(*per_lane):
        out = valid_list[per_lane[0]]
        for l in range(1, 4):
            out = jnp.where(lane == l, valid_list[per_lane[l]], out)
        return out

    groups = [
        (keys_values, valid_list[0]),
        (jnp.concatenate([along, cross, second, third], axis=1),
         jnp.concatenate([offset_of(3, 1, 3, 1), offset_of(4, 4, 2, 2), offset_of(1, 3, 1, 4),
                          offset_of(2, 2, 4, 3)])),
    ]
    anchor_valid = (place != anchor) & (row_ids < lengths[anchor])
    heads = [slice(h * HG * DH, (h + 1) * HG * DH) for h in range(H // HG)]
    query_heads = [queries[:, cols].reshape(tok_rows, HG, DH) for cols in heads]
    states = [None] * len(heads)
    for group_kv, group_valid in groups:
        for h, cols in enumerate(heads):
            states[h] = attend(query_heads[h], group_kv[:, :, cols], group_valid, states[h])
    anchor_kv, states = lax.optimization_barrier((anchor_kv, states))
    pieces = []
    for h, cols in enumerate(heads):
        top, total, out = attend(query_heads[h], anchor_kv[:, :, cols], anchor_valid, states[h])
        blended = out / total
        pieces.append(jnp.transpose(blended, (1, 0, 2)).reshape(tok_rows, HG * DH))
    attended = jnp.concatenate(pieces, axis=1)
    attended = jnp.where(row_ids[:, None] < lengths[place], attended, 0.0).astype(jnp.bfloat16)
    features = frames.astype(jnp.float32)
    squares = jnp.mean(features * features, axis=-1, keepdims=True)
    normed = features * lax.rsqrt(squares + 1e-06) * norm_gain
    activated = jax.nn.silu(normed).astype(jnp.bfloat16)
    stacked = jnp.concatenate([past_frames, activated], axis=0)
    extended = extended_2(stacked, (("span", 1),), 1)
    padded = jnp.pad(extended, ((0, 0), (0, 0), (1, 1), (0, 0)))
    frame_count = frames.shape[0]
    rows_here = frames.shape[1]
    col_count = frames.shape[2]
    channels = frames.shape[3]
    windows = []
    for frame_tap in range(3):
        for row_tap in range(3):
            for col_tap in range(3):
                windows.append(
                    padded[
                        frame_tap : frame_tap + frame_count,
                        row_tap : row_tap + rows_here,
                        col_tap : col_tap + col_count,
                        :,
                    ]
                )
    columns = jnp.concatenate(windows, axis=-1).reshape(-1, 27 * channels)
    convolved = jnp.dot(
        columns, conv_weight.reshape(27 * channels, channels), preferred_element_type=jnp.float32
    )
    decoded = features + conv_bias + convolved.reshape(frame_count, rows_here, col_count, channels)
    return (attended, decoded.astype(jnp.bfloat16))


def solution(mesh):
    placed = (
        P(("group", "span"), None),
        P(None, ("group", "span"), None),
        P("group"),
        P("group", None),
        P("group"),
        P("group", "span", None, None),
        P("group", "span", None, None),
        P(),
        P(),
        P(),
    )
    return jax.shard_map(
        shards,
        mesh=mesh,
        in_specs=placed,
        out_specs=(P(("group", "span"), None), P("group", "span", None, None)),
        check_vma=False,
    )
```

```python
import jax
import jax.numpy as jnp
from jax import lax
from jax.sharding import PartitionSpec as P

H = 20
DH = 128
WIN = 4
HG = 20


def spread(block, axis, source):
    block = jnp.where(lax.axis_index(axis) == source, block, jnp.zeros_like(block))
    return lax.psum(block, axis)


def extended_2(block, sides, width):
    for axis, dim in sides:
        count = lax.axis_size(axis)
        forward = [(i, i + 1) for i in range(count - 1)]
        backward = [(target, source) for source, target in forward]
        low = lax.ppermute(
            lax.slice_in_dim(block, block.shape[dim] - width, None, axis=dim), axis, forward
        )
        high = lax.ppermute(lax.slice_in_dim(block, 0, width, axis=dim), axis, backward)
        block = jnp.concatenate([low, block, high], axis=dim)
    return block


def move(value, pairs):
    return lax.ppermute(value, "span", pairs)


def window_blocks(kv, devices):
    rows = devices // 4
    lane = lax.axis_index("span") % 4

    def at(r, l):
        return 4 * (r % rows) + l

    def pairs(*moves):
        return [(at(r, a), at(r + step, b)) for a, b, step in moves for r in range(rows)]

    def pick(*options):
        out = options[0]
        for l in range(1, 4):
            out = jnp.where(lane == l, options[l], out)
        return out

    cross = move(kv, pairs((0, 2, 0), (1, 3, 0), (2, 1, 0)))
    along = move(kv, pairs((0, 1, 0), (2, 3, 0), (1, 0, 1), (3, 2, 1)))
    second = move(pick(cross, cross, along, cross), pairs((3, 2, 0), (2, 0, 0), (1, 1, 1)))
    third = move(pick(second, second, cross, cross), pairs((0, 1, 0), (1, 0, 0), (2, 3, 0)))
    return along, cross, second, third


def part_stats(q, k, valid, scale):
    scores = jnp.einsum("qhd,khd->hqk", q, k, preferred_element_type=jnp.float32) * scale
    return jnp.where(valid[None, None, :], scores, -jnp.inf)


def weighted(weights, values):
    return jnp.einsum(
        "hqk,khd->hqd", weights.astype(jnp.bfloat16), values, preferred_element_type=jnp.float32
    )


def attend(q, kv, valid, state):
    k = kv[0].reshape(-1, HG, DH)
    v = kv[1].reshape(-1, HG, DH)
    scores = part_stats(q, k, valid, DH ** (-0.5))
    top = jnp.max(scores, axis=-1, keepdims=True)
    if state is not None:
        top = jnp.maximum(state[0], top)
    weights = jnp.exp(scores - top)
    total = jnp.sum(weights, axis=-1, keepdims=True)
    out = weighted(weights, v)
    if state is not None:
        rescale = jnp.exp(state[0] - top)
        total = state[1] * rescale + total
        out = state[2] * rescale + out
    return top, total, out


def shards(
    queries,
    keys_values,
    owner,
    span_mask,
    lengths,
    frames,
    past_frames,
    norm_gain,
    conv_weight,
    conv_bias,
):
    devices = lax.axis_size("span")
    place = lax.axis_index("span")
    anchor = owner[0]
    position = (place - anchor - 1) % devices
    tok_rows = queries.shape[0]
    row_ids = jnp.arange(tok_rows, dtype=jnp.int32)
    is_anchor = place == anchor
    masked = jnp.where(is_anchor, keys_values, jnp.zeros_like(keys_values))
    anchor_kv = lax.psum(masked, "span")
    sent = jnp.where(is_anchor, lax.optimization_barrier(masked), keys_values)
    along, cross, second, third = window_blocks(sent, devices)
    valid_list = [row_ids < lengths[place]]
    for offset in range(1, WIN):
        source = (place - offset) % devices
        allowed = (position >= offset) & (span_mask[position, offset - 1] == 1)
        valid_list.append(allowed & (row_ids < lengths[source]))
    valid_list.append(jnp.zeros_like(valid_list[0]))
    lane = place % 4

    def offset_of(*per_lane):
        out = valid_list[per_lane[0]]
        for l in range(1, 4):
            out = jnp.where(lane == l, valid_list[per_lane[l]], out)
        return out

    groups = [
        (jnp.concatenate([keys_values, along], axis=1),
         jnp.concatenate([valid_list[0], offset_of(3, 1, 3, 1)])),
        (jnp.concatenate([cross, second], axis=1),
         jnp.concatenate([offset_of(4, 4, 2, 2), offset_of(1, 3, 1, 4)])),
        (third, offset_of(2, 2, 4, 3)),
    ]
    anchor_valid = (place != anchor) & (row_ids < lengths[anchor])
    heads = [slice(h * HG * DH, (h + 1) * HG * DH) for h in range(H // HG)]
    query_heads = [queries[:, cols].reshape(tok_rows, HG, DH) for cols in heads]
    states = [None] * len(heads)
    for group_kv, group_valid in groups:
        for h, cols in enumerate(heads):
            states[h] = attend(query_heads[h], group_kv[:, :, cols], group_valid, states[h])
    anchor_kv, states = lax.optimization_barrier((anchor_kv, states))
    pieces = []
    for h, cols in enumerate(heads):
        top, total, out = attend(query_heads[h], anchor_kv[:, :, cols], anchor_valid, states[h])
        blended = out / total
        pieces.append(jnp.transpose(blended, (1, 0, 2)).reshape(tok_rows, HG * DH))
    attended = jnp.concatenate(pieces, axis=1)
    attended = jnp.where(row_ids[:, None] < lengths[place], attended, 0.0).astype(jnp.bfloat16)
    features = frames.astype(jnp.float32)
    squares = jnp.mean(features * features, axis=-1, keepdims=True)
    normed = features * lax.rsqrt(squares + 1e-06) * norm_gain
    activated = jax.nn.silu(normed).astype(jnp.bfloat16)
    stacked = jnp.concatenate([past_frames, activated], axis=0)
    extended = extended_2(stacked, (("span", 1),), 1)
    padded = jnp.pad(extended, ((0, 0), (0, 0), (1, 1), (0, 0)))
    frame_count = frames.shape[0]
    rows_here = frames.shape[1]
    col_count = frames.shape[2]
    channels = frames.shape[3]
    windows = []
    for frame_tap in range(3):
        for row_tap in range(3):
            for col_tap in range(3):
                windows.append(
                    padded[
                        frame_tap : frame_tap + frame_count,
                        row_tap : row_tap + rows_here,
                        col_tap : col_tap + col_count,
                        :,
                    ]
                )
    columns = jnp.concatenate(windows, axis=-1).reshape(-1, 27 * channels)
    convolved = jnp.dot(
        columns, conv_weight.reshape(27 * channels, channels), preferred_element_type=jnp.float32
    )
    decoded = features + conv_bias + convolved.reshape(frame_count, rows_here, col_count, channels)
    return (attended, decoded.astype(jnp.bfloat16))


def solution(mesh):
    placed = (
        P(("group", "span"), None),
        P(None, ("group", "span"), None),
        P("group"),
        P("group", None),
        P("group"),
        P("group", "span", None, None),
        P("group", "span", None, None),
        P(),
        P(),
        P(),
    )
    return jax.shard_map(
        shards,
        mesh=mesh,
        in_specs=placed,
        out_specs=(P(("group", "span"), None), P("group", "span", None, None)),
        check_vma=False,
    )
```

```python
import jax
import jax.numpy as jnp
from jax import lax
from jax.sharding import PartitionSpec as P

H = 20
DH = 128
WIN = 4
HG = 20


def spread(block, axis, source):
    block = jnp.where(lax.axis_index(axis) == source, block, jnp.zeros_like(block))
    return lax.psum(block, axis)


def extended_2(block, sides, width):
    for axis, dim in sides:
        count = lax.axis_size(axis)
        forward = [(i, i + 1) for i in range(count - 1)]
        backward = [(target, source) for source, target in forward]
        low = lax.ppermute(
            lax.slice_in_dim(block, block.shape[dim] - width, None, axis=dim), axis, forward
        )
        high = lax.ppermute(lax.slice_in_dim(block, 0, width, axis=dim), axis, backward)
        block = jnp.concatenate([low, block, high], axis=dim)
    return block


def move(value, pairs):
    return lax.ppermute(value, "span", pairs)


def window_blocks(kv, devices):
    rows = devices // 4
    lane = lax.axis_index("span") % 4

    def at(r, l):
        return 4 * (r % rows) + l

    def pairs(*moves):
        return [(at(r, a), at(r + step, b)) for a, b, step in moves for r in range(rows)]

    def pick(*options):
        out = options[0]
        for l in range(1, 4):
            out = jnp.where(lane == l, options[l], out)
        return out

    cross = move(kv, pairs((0, 2, 0), (1, 3, 0), (2, 1, 0)))
    along = move(kv, pairs((0, 1, 0), (2, 3, 0), (1, 0, 1), (3, 2, 1)))
    second = move(pick(cross, cross, along, cross), pairs((3, 2, 0), (2, 0, 0), (1, 1, 1)))
    third = move(pick(second, second, cross, cross), pairs((0, 1, 0), (1, 0, 0), (2, 3, 0)))
    return along, cross, second, third


def part_stats(q, k, valid, scale):
    scores = jnp.einsum("qhd,khd->hqk", q, k, preferred_element_type=jnp.float32) * scale
    return jnp.where(valid[None, None, :], scores, -jnp.inf)


def weighted(weights, values):
    return jnp.einsum(
        "hqk,khd->hqd", weights.astype(jnp.bfloat16), values, preferred_element_type=jnp.float32
    )


def attend(q, blocks, state):
    scores = [
        part_stats(q, kv[0].reshape(-1, HG, DH), valid, DH ** (-0.5)) for kv, valid in blocks
    ]
    tops = [jnp.max(s, axis=-1, keepdims=True) for s in scores]
    if state is not None:
        tops.append(state[0])
    top = tops[0]
    for t in tops[1:]:
        top = jnp.maximum(top, t)
    total = None
    out = None
    for s, (kv, _) in zip(scores, blocks):
        weights = jnp.exp(s - top)
        part_total = jnp.sum(weights, axis=-1, keepdims=True)
        part_out = weighted(weights, kv[1].reshape(-1, HG, DH))
        total = part_total if total is None else total + part_total
        out = part_out if out is None else out + part_out
    if state is not None:
        rescale = jnp.exp(state[0] - top)
        total = state[1] * rescale + total
        out = state[2] * rescale + out
    return top, total, out


def shards(
    queries,
    keys_values,
    owner,
    span_mask,
    lengths,
    frames,
    past_frames,
    norm_gain,
    conv_weight,
    conv_bias,
):
    devices = lax.axis_size("span")
    place = lax.axis_index("span")
    anchor = owner[0]
    position = (place - anchor - 1) % devices
    tok_rows = queries.shape[0]
    row_ids = jnp.arange(tok_rows, dtype=jnp.int32)
    is_anchor = place == anchor
    masked = jnp.where(is_anchor, keys_values, jnp.zeros_like(keys_values))
    anchor_kv = lax.psum(masked, "span")
    sent = jnp.where(is_anchor, lax.optimization_barrier(masked), keys_values)
    along, cross, second, third = window_blocks(sent, devices)
    valid_list = [row_ids < lengths[place]]
    for offset in range(1, WIN):
        source = (place - offset) % devices
        allowed = (position >= offset) & (span_mask[position, offset - 1] == 1)
        valid_list.append(allowed & (row_ids < lengths[source]))
    valid_list.append(jnp.zeros_like(valid_list[0]))
    lane = place % 4

    def offset_of(*per_lane):
        out = valid_list[per_lane[0]]
        for l in range(1, 4):
            out = jnp.where(lane == l, valid_list[per_lane[l]], out)
        return out

    groups = [
        [(keys_values, valid_list[0]), (along, offset_of(3, 1, 3, 1))],
        [(cross, offset_of(4, 4, 2, 2)), (second, offset_of(1, 3, 1, 4))],
        [(third, offset_of(2, 2, 4, 3))],
    ]
    anchor_valid = (place != anchor) & (row_ids < lengths[anchor])
    heads = [slice(h * HG * DH, (h + 1) * HG * DH) for h in range(H // HG)]
    query_heads = [queries[:, cols].reshape(tok_rows, HG, DH) for cols in heads]
    states = [None] * len(heads)
    for group in groups:
        for h, cols in enumerate(heads):
            states[h] = attend(
                query_heads[h], [(kv[:, :, cols], valid) for kv, valid in group], states[h]
            )
    anchor_kv, states = lax.optimization_barrier((anchor_kv, states))
    pieces = []
    for h, cols in enumerate(heads):
        top, total, out = attend(query_heads[h], [(anchor_kv[:, :, cols], anchor_valid)], states[h])
        blended = out / total
        pieces.append(jnp.transpose(blended, (1, 0, 2)).reshape(tok_rows, HG * DH))
    attended = jnp.concatenate(pieces, axis=1)
    attended = jnp.where(row_ids[:, None] < lengths[place], attended, 0.0).astype(jnp.bfloat16)
    features = frames.astype(jnp.float32)
    squares = jnp.mean(features * features, axis=-1, keepdims=True)
    normed = features * lax.rsqrt(squares + 1e-06) * norm_gain
    activated = jax.nn.silu(normed).astype(jnp.bfloat16)
    stacked = jnp.concatenate([past_frames, activated], axis=0)
    extended = extended_2(stacked, (("span", 1),), 1)
    padded = jnp.pad(extended, ((0, 0), (0, 0), (1, 1), (0, 0)))
    frame_count = frames.shape[0]
    rows_here = frames.shape[1]
    col_count = frames.shape[2]
    channels = frames.shape[3]
    windows = []
    for frame_tap in range(3):
        for row_tap in range(3):
            for col_tap in range(3):
                windows.append(
                    padded[
                        frame_tap : frame_tap + frame_count,
                        row_tap : row_tap + rows_here,
                        col_tap : col_tap + col_count,
                        :,
                    ]
                )
    columns = jnp.concatenate(windows, axis=-1).reshape(-1, 27 * channels)
    convolved = jnp.dot(
        columns, conv_weight.reshape(27 * channels, channels), preferred_element_type=jnp.float32
    )
    decoded = features + conv_bias + convolved.reshape(frame_count, rows_here, col_count, channels)
    return (attended, decoded.astype(jnp.bfloat16))


def solution(mesh):
    placed = (
        P(("group", "span"), None),
        P(None, ("group", "span"), None),
        P("group"),
        P("group", None),
        P("group"),
        P("group", "span", None, None),
        P("group", "span", None, None),
        P(),
        P(),
        P(),
    )
    return jax.shard_map(
        shards,
        mesh=mesh,
        in_specs=placed,
        out_specs=(P(("group", "span"), None), P("group", "span", None, None)),
        check_vma=False,
    )
```

```python
import jax
import jax.numpy as jnp
from jax import lax
from jax.sharding import PartitionSpec as P

H = 20
DH = 128
WIN = 4
HG = 20


def spread(block, axis, source):
    block = jnp.where(lax.axis_index(axis) == source, block, jnp.zeros_like(block))
    return lax.psum(block, axis)


def extended_2(block, sides, width):
    for axis, dim in sides:
        count = lax.axis_size(axis)
        forward = [(i, i + 1) for i in range(count - 1)]
        backward = [(target, source) for source, target in forward]
        low = lax.ppermute(
            lax.slice_in_dim(block, block.shape[dim] - width, None, axis=dim), axis, forward
        )
        high = lax.ppermute(lax.slice_in_dim(block, 0, width, axis=dim), axis, backward)
        block = jnp.concatenate([low, block, high], axis=dim)
    return block


def move(value, pairs):
    return lax.ppermute(value, "span", pairs)


def window_blocks(kv, devices):
    rows = devices // 4
    lane = lax.axis_index("span") % 4

    def at(r, l):
        return 4 * (r % rows) + l

    def pairs(*moves):
        return [(at(r, a), at(r + step, b)) for a, b, step in moves for r in range(rows)]

    def pick(*options):
        out = options[0]
        for l in range(1, 4):
            out = jnp.where(lane == l, options[l], out)
        return out

    cross = move(kv, pairs((0, 2, 0), (1, 3, 0), (2, 1, 0)))
    along = move(kv, pairs((0, 1, 0), (2, 3, 0), (1, 0, 1), (3, 2, 1)))
    second = move(pick(cross, cross, along, cross), pairs((3, 2, 0), (2, 0, 0), (1, 1, 1)))

    def round_three(ready):
        payload, ready = lax.optimization_barrier((pick(second, second, cross, cross), ready))
        return move(payload, pairs((0, 1, 0), (1, 0, 0), (2, 3, 0))), ready

    return along, cross, second, round_three


def part_stats(q, k, valid, scale):
    scores = jnp.einsum("qhd,khd->hqk", q, k, preferred_element_type=jnp.float32) * scale
    return jnp.where(valid[None, None, :], scores, -jnp.inf)


def weighted(weights, values):
    return jnp.einsum(
        "hqk,khd->hqd", weights.astype(jnp.bfloat16), values, preferred_element_type=jnp.float32
    )


def attend(q, blocks, state):
    scores = [
        part_stats(q, kv[0].reshape(-1, HG, DH), valid, DH ** (-0.5)) for kv, valid in blocks
    ]
    tops = [jnp.max(s, axis=-1, keepdims=True) for s in scores]
    if state is not None:
        tops.append(state[0])
    top = tops[0]
    for t in tops[1:]:
        top = jnp.maximum(top, t)
    total = None
    out = None
    for s, (kv, _) in zip(scores, blocks):
        weights = jnp.exp(s - top)
        part_total = jnp.sum(weights, axis=-1, keepdims=True)
        part_out = weighted(weights, kv[1].reshape(-1, HG, DH))
        total = part_total if total is None else total + part_total
        out = part_out if out is None else out + part_out
    if state is not None:
        rescale = jnp.exp(state[0] - top)
        total = state[1] * rescale + total
        out = state[2] * rescale + out
    return top, total, out


def shards(
    queries,
    keys_values,
    owner,
    span_mask,
    lengths,
    frames,
    past_frames,
    norm_gain,
    conv_weight,
    conv_bias,
):
    devices = lax.axis_size("span")
    place = lax.axis_index("span")
    anchor = owner[0]
    position = (place - anchor - 1) % devices
    tok_rows = queries.shape[0]
    row_ids = jnp.arange(tok_rows, dtype=jnp.int32)
    is_anchor = place == anchor
    masked = jnp.where(is_anchor, keys_values, jnp.zeros_like(keys_values))
    anchor_kv = lax.psum(masked, "span")
    sent = jnp.where(is_anchor, lax.optimization_barrier(masked), keys_values)
    along, cross, second, round_three = window_blocks(sent, devices)
    valid_list = [row_ids < lengths[place]]
    for offset in range(1, WIN):
        source = (place - offset) % devices
        allowed = (position >= offset) & (span_mask[position, offset - 1] == 1)
        valid_list.append(allowed & (row_ids < lengths[source]))
    valid_list.append(jnp.zeros_like(valid_list[0]))
    lane = place % 4

    def offset_of(*per_lane):
        out = valid_list[per_lane[0]]
        for l in range(1, 4):
            out = jnp.where(lane == l, valid_list[per_lane[l]], out)
        return out

    groups = [
        [(keys_values, valid_list[0]), (along, offset_of(3, 1, 3, 1))],
        [(cross, offset_of(4, 4, 2, 2)), (second, offset_of(1, 3, 1, 4))],
    ]
    anchor_valid = (place != anchor) & (row_ids < lengths[anchor])
    heads = [slice(h * HG * DH, (h + 1) * HG * DH) for h in range(H // HG)]
    query_heads = [queries[:, cols].reshape(tok_rows, HG, DH) for cols in heads]
    states = [None] * len(heads)
    for group in groups:
        for h, cols in enumerate(heads):
            states[h] = attend(
                query_heads[h], [(kv[:, :, cols], valid) for kv, valid in group], states[h]
            )
    third, states = round_three(states)
    third_valid = offset_of(2, 2, 4, 3)
    for h, cols in enumerate(heads):
        states[h] = attend(query_heads[h], [(third[:, :, cols], third_valid)], states[h])
    anchor_kv, states = lax.optimization_barrier((anchor_kv, states))
    pieces = []
    for h, cols in enumerate(heads):
        top, total, out = attend(query_heads[h], [(anchor_kv[:, :, cols], anchor_valid)], states[h])
        blended = out / total
        pieces.append(jnp.transpose(blended, (1, 0, 2)).reshape(tok_rows, HG * DH))
    attended = jnp.concatenate(pieces, axis=1)
    attended = jnp.where(row_ids[:, None] < lengths[place], attended, 0.0).astype(jnp.bfloat16)
    features = frames.astype(jnp.float32)
    squares = jnp.mean(features * features, axis=-1, keepdims=True)
    normed = features * lax.rsqrt(squares + 1e-06) * norm_gain
    activated = jax.nn.silu(normed).astype(jnp.bfloat16)
    stacked = jnp.concatenate([past_frames, activated], axis=0)
    extended = extended_2(stacked, (("span", 1),), 1)
    padded = jnp.pad(extended, ((0, 0), (0, 0), (1, 1), (0, 0)))
    frame_count = frames.shape[0]
    rows_here = frames.shape[1]
    col_count = frames.shape[2]
    channels = frames.shape[3]
    windows = []
    for frame_tap in range(3):
        for row_tap in range(3):
            for col_tap in range(3):
                windows.append(
                    padded[
                        frame_tap : frame_tap + frame_count,
                        row_tap : row_tap + rows_here,
                        col_tap : col_tap + col_count,
                        :,
                    ]
                )
    columns = jnp.concatenate(windows, axis=-1).reshape(-1, 27 * channels)
    convolved = jnp.dot(
        columns, conv_weight.reshape(27 * channels, channels), preferred_element_type=jnp.float32
    )
    decoded = features + conv_bias + convolved.reshape(frame_count, rows_here, col_count, channels)
    return (attended, decoded.astype(jnp.bfloat16))


def solution(mesh):
    placed = (
        P(("group", "span"), None),
        P(None, ("group", "span"), None),
        P("group"),
        P("group", None),
        P("group"),
        P("group", "span", None, None),
        P("group", "span", None, None),
        P(),
        P(),
        P(),
    )
    return jax.shard_map(
        shards,
        mesh=mesh,
        in_specs=placed,
        out_specs=(P(("group", "span"), None), P("group", "span", None, None)),
        check_vma=False,
    )
```

```python
import jax
import jax.numpy as jnp
from jax import lax
from jax.sharding import PartitionSpec as P

H = 20
DH = 128
WIN = 4
HG = 20


def spread(block, axis, source):
    block = jnp.where(lax.axis_index(axis) == source, block, jnp.zeros_like(block))
    return lax.psum(block, axis)


def extended_2(block, sides, width):
    for axis, dim in sides:
        count = lax.axis_size(axis)
        forward = [(i, i + 1) for i in range(count - 1)]
        backward = [(target, source) for source, target in forward]
        low = lax.ppermute(
            lax.slice_in_dim(block, block.shape[dim] - width, None, axis=dim), axis, forward
        )
        high = lax.ppermute(lax.slice_in_dim(block, 0, width, axis=dim), axis, backward)
        block = jnp.concatenate([low, block, high], axis=dim)
    return block


def move(value, pairs):
    return lax.ppermute(value, "span", pairs)


def window_blocks(kv, devices):
    rows = devices // 4
    lane = lax.axis_index("span") % 4

    def at(r, l):
        return 4 * (r % rows) + l

    def pairs(*moves):
        return [(at(r, a), at(r + step, b)) for a, b, step in moves for r in range(rows)]

    def pick(*options):
        out = options[0]
        for l in range(1, 4):
            out = jnp.where(lane == l, options[l], out)
        return out

    cross = move(kv, pairs((0, 2, 0), (1, 3, 0), (2, 1, 0)))
    along = move(kv, pairs((0, 1, 0), (2, 3, 0), (1, 0, 1), (3, 2, 1)))
    second = move(pick(cross, cross, along, cross), pairs((3, 2, 0), (2, 0, 0), (1, 1, 1)))
    third = move(pick(second, second, cross, cross), pairs((0, 1, 0), (1, 0, 0), (2, 3, 0)))
    return along, cross, second, third


def part_stats(q, k, valid, scale):
    scores = jnp.einsum("qhd,khd->hqk", q, k, preferred_element_type=jnp.float32) * scale
    return jnp.where(valid[None, None, :], scores, -jnp.inf)


def weighted(weights, values):
    return jnp.einsum(
        "hqk,khd->hqd", weights.astype(jnp.bfloat16), values, preferred_element_type=jnp.float32
    )


def attend(q, blocks, state):
    scores = [
        part_stats(q, kv[0].reshape(-1, HG, DH), valid, DH ** (-0.5)) for kv, valid in blocks
    ]
    tops = [jnp.max(s, axis=-1, keepdims=True) for s in scores]
    if state is not None:
        tops.append(state[0])
    top = tops[0]
    for t in tops[1:]:
        top = jnp.maximum(top, t)
    total = None
    out = None
    for s, (kv, _) in zip(scores, blocks):
        weights = jnp.exp(s - top)
        part_total = jnp.sum(weights, axis=-1, keepdims=True)
        part_out = weighted(weights, kv[1].reshape(-1, HG, DH))
        total = part_total if total is None else total + part_total
        out = part_out if out is None else out + part_out
    if state is not None:
        rescale = jnp.exp(state[0] - top)
        total = state[1] * rescale + total
        out = state[2] * rescale + out
    return top, total, out


def shards(
    queries,
    keys_values,
    owner,
    span_mask,
    lengths,
    frames,
    past_frames,
    norm_gain,
    conv_weight,
    conv_bias,
):
    devices = lax.axis_size("span")
    place = lax.axis_index("span")
    anchor = owner[0]
    position = (place - anchor - 1) % devices
    tok_rows = queries.shape[0]
    row_ids = jnp.arange(tok_rows, dtype=jnp.int32)
    is_anchor = place == anchor
    masked = jnp.where(is_anchor, keys_values, jnp.zeros_like(keys_values))
    anchor_kv = lax.psum(masked, "span")
    sent = jnp.where(is_anchor, lax.optimization_barrier(masked), keys_values)
    along, cross, second, third = window_blocks(sent, devices)
    valid_list = [row_ids < lengths[place]]
    for offset in range(1, WIN):
        source = (place - offset) % devices
        allowed = (position >= offset) & (span_mask[position, offset - 1] == 1)
        valid_list.append(allowed & (row_ids < lengths[source]))
    valid_list.append(jnp.zeros_like(valid_list[0]))
    lane = place % 4

    def offset_of(*per_lane):
        out = valid_list[per_lane[0]]
        for l in range(1, 4):
            out = jnp.where(lane == l, valid_list[per_lane[l]], out)
        return out

    early = jnp.where(lane < 2, second, cross)
    late = jnp.where(lane == 2, second, third)
    groups = [
        [(keys_values, valid_list[0]), (along, offset_of(3, 1, 3, 1))],
        [(early, offset_of(1, 3, 2, 2))],
        [(late, offset_of(2, 2, 1, 3))],
    ]
    anchor_valid = (place != anchor) & (row_ids < lengths[anchor])
    heads = [slice(h * HG * DH, (h + 1) * HG * DH) for h in range(H // HG)]
    query_heads = [queries[:, cols].reshape(tok_rows, HG, DH) for cols in heads]
    states = [None] * len(heads)
    for group in groups:
        for h, cols in enumerate(heads):
            states[h] = attend(
                query_heads[h], [(kv[:, :, cols], valid) for kv, valid in group], states[h]
            )
    anchor_kv, states = lax.optimization_barrier((anchor_kv, states))
    pieces = []
    for h, cols in enumerate(heads):
        top, total, out = attend(query_heads[h], [(anchor_kv[:, :, cols], anchor_valid)], states[h])
        blended = out / total
        pieces.append(jnp.transpose(blended, (1, 0, 2)).reshape(tok_rows, HG * DH))
    attended = jnp.concatenate(pieces, axis=1)
    attended = jnp.where(row_ids[:, None] < lengths[place], attended, 0.0).astype(jnp.bfloat16)
    features = frames.astype(jnp.float32)
    squares = jnp.mean(features * features, axis=-1, keepdims=True)
    normed = features * lax.rsqrt(squares + 1e-06) * norm_gain
    activated = jax.nn.silu(normed).astype(jnp.bfloat16)
    stacked = jnp.concatenate([past_frames, activated], axis=0)
    extended = extended_2(stacked, (("span", 1),), 1)
    padded = jnp.pad(extended, ((0, 0), (0, 0), (1, 1), (0, 0)))
    frame_count = frames.shape[0]
    rows_here = frames.shape[1]
    col_count = frames.shape[2]
    channels = frames.shape[3]
    windows = []
    for frame_tap in range(3):
        for row_tap in range(3):
            for col_tap in range(3):
                windows.append(
                    padded[
                        frame_tap : frame_tap + frame_count,
                        row_tap : row_tap + rows_here,
                        col_tap : col_tap + col_count,
                        :,
                    ]
                )
    columns = jnp.concatenate(windows, axis=-1).reshape(-1, 27 * channels)
    convolved = jnp.dot(
        columns, conv_weight.reshape(27 * channels, channels), preferred_element_type=jnp.float32
    )
    decoded = features + conv_bias + convolved.reshape(frame_count, rows_here, col_count, channels)
    return (attended, decoded.astype(jnp.bfloat16))


def solution(mesh):
    placed = (
        P(("group", "span"), None),
        P(None, ("group", "span"), None),
        P("group"),
        P("group", None),
        P("group"),
        P("group", "span", None, None),
        P("group", "span", None, None),
        P(),
        P(),
        P(),
    )
    return jax.shard_map(
        shards,
        mesh=mesh,
        in_specs=placed,
        out_specs=(P(("group", "span"), None), P("group", "span", None, None)),
        check_vma=False,
    )
```

```python
import jax
import jax.numpy as jnp
from jax import lax
from jax.sharding import PartitionSpec as P

H = 20
DH = 128
WIN = 4
HG = 20


def spread(block, axis, source):
    block = jnp.where(lax.axis_index(axis) == source, block, jnp.zeros_like(block))
    return lax.psum(block, axis)


def extended_2(block, sides, width):
    for axis, dim in sides:
        count = lax.axis_size(axis)
        forward = [(i, i + 1) for i in range(count - 1)]
        backward = [(target, source) for source, target in forward]
        low = lax.ppermute(
            lax.slice_in_dim(block, block.shape[dim] - width, None, axis=dim), axis, forward
        )
        high = lax.ppermute(lax.slice_in_dim(block, 0, width, axis=dim), axis, backward)
        block = jnp.concatenate([low, block, high], axis=dim)
    return block


def move(value, pairs):
    return lax.ppermute(value, "span", pairs)


def window_blocks(kv, devices):
    rows = devices // 4
    lane = lax.axis_index("span") % 4

    def at(r, l):
        return 4 * (r % rows) + l

    def pairs(*moves):
        return [(at(r, a), at(r + step, b)) for a, b, step in moves for r in range(rows)]

    def pick(*options):
        out = options[0]
        for l in range(1, 4):
            out = jnp.where(lane == l, options[l], out)
        return out

    cross = move(kv, pairs((0, 2, 0), (1, 3, 0), (2, 1, 0)))
    along = move(kv, pairs((0, 1, 0), (2, 3, 0), (1, 0, 1), (3, 2, 1)))
    second = move(pick(cross, cross, along, cross), pairs((3, 2, 0), (2, 0, 0), (1, 1, 1)))
    onchip = move(cross, pairs((2, 3, 0)))
    third = jnp.where(lane == 3, onchip, move(second, pairs((0, 1, 0), (1, 0, 0))))
    return along, cross, second, third


def part_stats(q, k, valid, scale):
    scores = jnp.einsum("qhd,khd->hqk", q, k, preferred_element_type=jnp.float32) * scale
    return jnp.where(valid[None, None, :], scores, -jnp.inf)


def weighted(weights, values):
    return jnp.einsum(
        "hqk,khd->hqd", weights.astype(jnp.bfloat16), values, preferred_element_type=jnp.float32
    )


def attend(q, blocks, state):
    scores = [
        part_stats(q, kv[0].reshape(-1, HG, DH), valid, DH ** (-0.5)) for kv, valid in blocks
    ]
    tops = [jnp.max(s, axis=-1, keepdims=True) for s in scores]
    if state is not None:
        tops.append(state[0])
    top = tops[0]
    for t in tops[1:]:
        top = jnp.maximum(top, t)
    total = None
    out = None
    for s, (kv, _) in zip(scores, blocks):
        weights = jnp.exp(s - top)
        part_total = jnp.sum(weights, axis=-1, keepdims=True)
        part_out = weighted(weights, kv[1].reshape(-1, HG, DH))
        total = part_total if total is None else total + part_total
        out = part_out if out is None else out + part_out
    if state is not None:
        rescale = jnp.exp(state[0] - top)
        total = state[1] * rescale + total
        out = state[2] * rescale + out
    return top, total, out


def shards(
    queries,
    keys_values,
    owner,
    span_mask,
    lengths,
    frames,
    past_frames,
    norm_gain,
    conv_weight,
    conv_bias,
):
    devices = lax.axis_size("span")
    place = lax.axis_index("span")
    anchor = owner[0]
    position = (place - anchor - 1) % devices
    tok_rows = queries.shape[0]
    row_ids = jnp.arange(tok_rows, dtype=jnp.int32)
    is_anchor = place == anchor
    masked = jnp.where(is_anchor, keys_values, jnp.zeros_like(keys_values))
    anchor_kv = lax.psum(masked, "span")
    sent = jnp.where(is_anchor, lax.optimization_barrier(masked), keys_values)
    along, cross, second, third = window_blocks(sent, devices)
    valid_list = [row_ids < lengths[place]]
    for offset in range(1, WIN):
        source = (place - offset) % devices
        allowed = (position >= offset) & (span_mask[position, offset - 1] == 1)
        valid_list.append(allowed & (row_ids < lengths[source]))
    valid_list.append(jnp.zeros_like(valid_list[0]))
    lane = place % 4

    def offset_of(*per_lane):
        out = valid_list[per_lane[0]]
        for l in range(1, 4):
            out = jnp.where(lane == l, valid_list[per_lane[l]], out)
        return out

    early = jnp.where(lane < 2, second, cross)
    late = jnp.where(lane == 2, second, third)
    groups = [
        [(keys_values, valid_list[0]), (along, offset_of(3, 1, 3, 1))],
        [(early, offset_of(1, 3, 2, 2))],
        [(late, offset_of(2, 2, 1, 3))],
    ]
    anchor_valid = (place != anchor) & (row_ids < lengths[anchor])
    heads = [slice(h * HG * DH, (h + 1) * HG * DH) for h in range(H // HG)]
    query_heads = [queries[:, cols].reshape(tok_rows, HG, DH) for cols in heads]
    states = [None] * len(heads)
    for group in groups:
        for h, cols in enumerate(heads):
            states[h] = attend(
                query_heads[h], [(kv[:, :, cols], valid) for kv, valid in group], states[h]
            )
    anchor_kv, states = lax.optimization_barrier((anchor_kv, states))
    pieces = []
    for h, cols in enumerate(heads):
        top, total, out = attend(query_heads[h], [(anchor_kv[:, :, cols], anchor_valid)], states[h])
        blended = out / total
        pieces.append(jnp.transpose(blended, (1, 0, 2)).reshape(tok_rows, HG * DH))
    attended = jnp.concatenate(pieces, axis=1)
    attended = jnp.where(row_ids[:, None] < lengths[place], attended, 0.0).astype(jnp.bfloat16)
    features = frames.astype(jnp.float32)
    squares = jnp.mean(features * features, axis=-1, keepdims=True)
    normed = features * lax.rsqrt(squares + 1e-06) * norm_gain
    activated = jax.nn.silu(normed).astype(jnp.bfloat16)
    stacked = jnp.concatenate([past_frames, activated], axis=0)
    extended = extended_2(stacked, (("span", 1),), 1)
    padded = jnp.pad(extended, ((0, 0), (0, 0), (1, 1), (0, 0)))
    frame_count = frames.shape[0]
    rows_here = frames.shape[1]
    col_count = frames.shape[2]
    channels = frames.shape[3]
    windows = []
    for frame_tap in range(3):
        for row_tap in range(3):
            for col_tap in range(3):
                windows.append(
                    padded[
                        frame_tap : frame_tap + frame_count,
                        row_tap : row_tap + rows_here,
                        col_tap : col_tap + col_count,
                        :,
                    ]
                )
    columns = jnp.concatenate(windows, axis=-1).reshape(-1, 27 * channels)
    convolved = jnp.dot(
        columns, conv_weight.reshape(27 * channels, channels), preferred_element_type=jnp.float32
    )
    decoded = features + conv_bias + convolved.reshape(frame_count, rows_here, col_count, channels)
    return (attended, decoded.astype(jnp.bfloat16))


def solution(mesh):
    placed = (
        P(("group", "span"), None),
        P(None, ("group", "span"), None),
        P("group"),
        P("group", None),
        P("group"),
        P("group", "span", None, None),
        P("group", "span", None, None),
        P(),
        P(),
        P(),
    )
    return jax.shard_map(
        shards,
        mesh=mesh,
        in_specs=placed,
        out_specs=(P(("group", "span"), None), P("group", "span", None, None)),
        check_vma=False,
    )
```

```python
import jax
import jax.numpy as jnp
from jax import lax
from jax.sharding import PartitionSpec as P

H = 20
DH = 128
WIN = 4
HG = 20


def spread(block, axis, source):
    block = jnp.where(lax.axis_index(axis) == source, block, jnp.zeros_like(block))
    return lax.psum(block, axis)


def extended_2(block, sides, width):
    for axis, dim in sides:
        count = lax.axis_size(axis)
        forward = [(i, i + 1) for i in range(count - 1)]
        backward = [(target, source) for source, target in forward]
        low = lax.ppermute(
            lax.slice_in_dim(block, block.shape[dim] - width, None, axis=dim), axis, forward
        )
        high = lax.ppermute(lax.slice_in_dim(block, 0, width, axis=dim), axis, backward)
        block = jnp.concatenate([low, block, high], axis=dim)
    return block


def move(value, pairs):
    return lax.ppermute(value, "span", pairs)


def window_blocks(kv, devices):
    rows = devices // 4
    lane = lax.axis_index("span") % 4

    def at(r, l):
        return 4 * (r % rows) + l

    def pairs(*moves):
        return [(at(r, a), at(r + step, b)) for a, b, step in moves for r in range(rows)]

    def pick(*options):
        out = options[0]
        for l in range(1, 4):
            out = jnp.where(lane == l, options[l], out)
        return out

    cross = move(kv, pairs((0, 2, 0), (1, 3, 0), (2, 1, 0)))
    along = move(kv, pairs((0, 1, 0), (2, 3, 0), (1, 0, 1), (3, 2, 1)))
    second = move(pick(cross, cross, along, cross), pairs((3, 2, 0), (2, 0, 0), (1, 1, 1)))
    third = move(pick(second, second, cross, cross), pairs((0, 1, 0), (1, 0, 0), (2, 3, 0)))
    return along, cross, second, third


def part_stats(q, k, valid, scale):
    scores = jnp.einsum("qhd,khd->hqk", q, k, preferred_element_type=jnp.float32) * scale
    return jnp.where(valid[None, None, :], scores, -jnp.inf)


def weighted(weights, values):
    return jnp.einsum(
        "hqk,khd->hqd", weights.astype(jnp.bfloat16), values, preferred_element_type=jnp.float32
    )


def attend(q, blocks, state):
    scores = [
        part_stats(q, kv[0].reshape(-1, HG, DH), valid, DH ** (-0.5)) for kv, valid in blocks
    ]
    tops = [jnp.max(s, axis=-1, keepdims=True) for s in scores]
    if state is not None:
        tops.append(state[0])
    top = tops[0]
    for t in tops[1:]:
        top = jnp.maximum(top, t)
    total = None
    out = None
    for s, (kv, _) in zip(scores, blocks):
        weights = jnp.exp(s - top)
        part_total = jnp.sum(weights, axis=-1, keepdims=True)
        part_out = weighted(weights, kv[1].reshape(-1, HG, DH))
        total = part_total if total is None else total + part_total
        out = part_out if out is None else out + part_out
    if state is not None:
        rescale = jnp.exp(state[0] - top)
        total = state[1] * rescale + total
        out = state[2] * rescale + out
    return top, total, out


def shards(
    queries,
    keys_values,
    owner,
    span_mask,
    lengths,
    frames,
    past_frames,
    norm_gain,
    conv_weight,
    conv_bias,
):
    devices = lax.axis_size("span")
    place = lax.axis_index("span")
    anchor = owner[0]
    position = (place - anchor - 1) % devices
    tok_rows = queries.shape[0]
    row_ids = jnp.arange(tok_rows, dtype=jnp.int32)
    is_anchor = place == anchor
    masked = jnp.where(is_anchor, keys_values, jnp.zeros_like(keys_values))
    anchor_kv = lax.psum(masked, "span")
    sent = jnp.where(is_anchor, lax.optimization_barrier(masked), keys_values)
    along, cross, second, third = window_blocks(sent, devices)
    valid_list = [row_ids < lengths[place]]
    for offset in range(1, WIN):
        source = (place - offset) % devices
        allowed = (position >= offset) & (span_mask[position, offset - 1] == 1)
        valid_list.append(allowed & (row_ids < lengths[source]))
    valid_list.append(jnp.zeros_like(valid_list[0]))
    lane = place % 4

    def offset_of(*per_lane):
        out = valid_list[per_lane[0]]
        for l in range(1, 4):
            out = jnp.where(lane == l, valid_list[per_lane[l]], out)
        return out

    early = jnp.where(lane < 2, second, cross)
    late = jnp.where(lane == 2, second, third)
    groups = [
        [(keys_values, valid_list[0]), (along, offset_of(3, 1, 3, 1))],
        [(early, offset_of(1, 3, 2, 2))],
    ]
    late_valid = offset_of(2, 2, 1, 3)
    anchor_valid = (place != anchor) & (row_ids < lengths[anchor])
    heads = [slice(h * HG * DH, (h + 1) * HG * DH) for h in range(H // HG)]
    query_heads = [queries[:, cols].reshape(tok_rows, HG, DH) for cols in heads]
    states = [None] * len(heads)
    for group in groups:
        for h, cols in enumerate(heads):
            states[h] = attend(
                query_heads[h], [(kv[:, :, cols], valid) for kv, valid in group], states[h]
            )
    anchor_kv, states = lax.optimization_barrier((anchor_kv, states))
    pieces = []
    for h, cols in enumerate(heads):
        last = [(late[:, :, cols], late_valid), (anchor_kv[:, :, cols], anchor_valid)]
        top, total, out = attend(query_heads[h], last, states[h])
        blended = out / total
        pieces.append(jnp.transpose(blended, (1, 0, 2)).reshape(tok_rows, HG * DH))
    attended = jnp.concatenate(pieces, axis=1)
    attended = jnp.where(row_ids[:, None] < lengths[place], attended, 0.0).astype(jnp.bfloat16)
    features = frames.astype(jnp.float32)
    squares = jnp.mean(features * features, axis=-1, keepdims=True)
    normed = features * lax.rsqrt(squares + 1e-06) * norm_gain
    activated = jax.nn.silu(normed).astype(jnp.bfloat16)
    stacked = jnp.concatenate([past_frames, activated], axis=0)
    extended = extended_2(stacked, (("span", 1),), 1)
    padded = jnp.pad(extended, ((0, 0), (0, 0), (1, 1), (0, 0)))
    frame_count = frames.shape[0]
    rows_here = frames.shape[1]
    col_count = frames.shape[2]
    channels = frames.shape[3]
    windows = []
    for frame_tap in range(3):
        for row_tap in range(3):
            for col_tap in range(3):
                windows.append(
                    padded[
                        frame_tap : frame_tap + frame_count,
                        row_tap : row_tap + rows_here,
                        col_tap : col_tap + col_count,
                        :,
                    ]
                )
    columns = jnp.concatenate(windows, axis=-1).reshape(-1, 27 * channels)
    convolved = jnp.dot(
        columns, conv_weight.reshape(27 * channels, channels), preferred_element_type=jnp.float32
    )
    decoded = features + conv_bias + convolved.reshape(frame_count, rows_here, col_count, channels)
    return (attended, decoded.astype(jnp.bfloat16))


def solution(mesh):
    placed = (
        P(("group", "span"), None),
        P(None, ("group", "span"), None),
        P("group"),
        P("group", None),
        P("group"),
        P("group", "span", None, None),
        P("group", "span", None, None),
        P(),
        P(),
        P(),
    )
    return jax.shard_map(
        shards,
        mesh=mesh,
        in_specs=placed,
        out_specs=(P(("group", "span"), None), P("group", "span", None, None)),
        check_vma=False,
    )
```

```python
import jax
import jax.numpy as jnp
from jax import lax
from jax.sharding import PartitionSpec as P

H = 20
DH = 128
WIN = 4
HG = 20


def spread(block, axis, source):
    block = jnp.where(lax.axis_index(axis) == source, block, jnp.zeros_like(block))
    return lax.psum(block, axis)


def extended_2(block, sides, width):
    for axis, dim in sides:
        count = lax.axis_size(axis)
        forward = [(i, i + 1) for i in range(count - 1)]
        backward = [(target, source) for source, target in forward]
        low = lax.ppermute(
            lax.slice_in_dim(block, block.shape[dim] - width, None, axis=dim), axis, forward
        )
        high = lax.ppermute(lax.slice_in_dim(block, 0, width, axis=dim), axis, backward)
        block = jnp.concatenate([low, block, high], axis=dim)
    return block


def move(value, pairs):
    return lax.ppermute(value, "span", pairs)


def window_blocks(kv, devices):
    rows = devices // 4
    lane = lax.axis_index("span") % 4

    def at(r, l):
        return 4 * (r % rows) + l

    def pairs(*moves):
        return [(at(r, a), at(r + step, b)) for a, b, step in moves for r in range(rows)]

    def pick(*options):
        out = options[0]
        for l in range(1, 4):
            out = jnp.where(lane == l, options[l], out)
        return out

    cross = move(kv, pairs((0, 2, 0), (1, 3, 0), (2, 1, 0)))
    along = move(kv, pairs((0, 1, 0), (2, 3, 0), (1, 0, 1), (3, 2, 1)))
    second = move(pick(cross, cross, along, cross), pairs((3, 2, 0), (2, 0, 0), (1, 1, 1)))
    third = move(pick(second, second, cross, cross), pairs((0, 1, 0), (1, 0, 0), (2, 3, 0)))
    return along, cross, second, third


def part_stats(q, k, valid, scale):
    scores = jnp.einsum("qhd,khd->hqk", q, k, preferred_element_type=jnp.float32) * scale
    return jnp.where(valid[None, None, :], scores, -jnp.inf)


def weighted(weights, values):
    return jnp.einsum(
        "hqk,khd->hqd", weights.astype(jnp.bfloat16), values, preferred_element_type=jnp.float32
    )


def attend(q, blocks, state):
    scores = [
        part_stats(q, kv[0].reshape(-1, HG, DH), valid, DH ** (-0.5)) for kv, valid in blocks
    ]
    tops = [jnp.max(s, axis=-1, keepdims=True) for s in scores]
    if state is not None:
        tops.append(state[0])
    top = tops[0]
    for t in tops[1:]:
        top = jnp.maximum(top, t)
    total = None
    out = None
    for s, (kv, _) in zip(scores, blocks):
        weights = jnp.exp(s - top)
        part_total = jnp.sum(weights, axis=-1, keepdims=True)
        part_out = weighted(weights, kv[1].reshape(-1, HG, DH))
        total = part_total if total is None else total + part_total
        out = part_out if out is None else out + part_out
    if state is not None:
        rescale = jnp.exp(state[0] - top)
        total = state[1] * rescale + total
        out = state[2] * rescale + out
    return top, total, out


def shards(
    queries,
    keys_values,
    owner,
    span_mask,
    lengths,
    frames,
    past_frames,
    norm_gain,
    conv_weight,
    conv_bias,
):
    devices = lax.axis_size("span")
    place = lax.axis_index("span")
    anchor = owner[0]
    position = (place - anchor - 1) % devices
    tok_rows = queries.shape[0]
    row_ids = jnp.arange(tok_rows, dtype=jnp.int32)
    is_anchor = place == anchor
    masked = jnp.where(is_anchor, keys_values, jnp.zeros_like(keys_values))
    anchor_kv = lax.psum(masked, "span")
    along, cross, second, third = window_blocks(keys_values, devices)
    valid_list = [row_ids < lengths[place]]
    for offset in range(1, WIN):
        source = (place - offset) % devices
        allowed = (position >= offset) & (span_mask[position, offset - 1] == 1)
        valid_list.append(allowed & (row_ids < lengths[source]))
    valid_list.append(jnp.zeros_like(valid_list[0]))
    lane = place % 4

    def offset_of(*per_lane):
        out = valid_list[per_lane[0]]
        for l in range(1, 4):
            out = jnp.where(lane == l, valid_list[per_lane[l]], out)
        return out

    early = jnp.where(lane < 2, second, cross)
    late = jnp.where(lane == 2, second, third)
    groups = [
        [(keys_values, valid_list[0]), (along, offset_of(3, 1, 3, 1))],
        [(early, offset_of(1, 3, 2, 2))],
        [(late, offset_of(2, 2, 1, 3))],
    ]
    anchor_valid = (place != anchor) & (row_ids < lengths[anchor])
    heads = [slice(h * HG * DH, (h + 1) * HG * DH) for h in range(H // HG)]
    query_heads = [queries[:, cols].reshape(tok_rows, HG, DH) for cols in heads]
    states = [None] * len(heads)
    for group in groups:
        for h, cols in enumerate(heads):
            states[h] = attend(
                query_heads[h], [(kv[:, :, cols], valid) for kv, valid in group], states[h]
            )
    anchor_kv, states = lax.optimization_barrier((anchor_kv, states))
    pieces = []
    for h, cols in enumerate(heads):
        top, total, out = attend(query_heads[h], [(anchor_kv[:, :, cols], anchor_valid)], states[h])
        blended = out / total
        pieces.append(jnp.transpose(blended, (1, 0, 2)).reshape(tok_rows, HG * DH))
    attended = jnp.concatenate(pieces, axis=1)
    attended = jnp.where(row_ids[:, None] < lengths[place], attended, 0.0).astype(jnp.bfloat16)
    features = frames.astype(jnp.float32)
    squares = jnp.mean(features * features, axis=-1, keepdims=True)
    normed = features * lax.rsqrt(squares + 1e-06) * norm_gain
    activated = jax.nn.silu(normed).astype(jnp.bfloat16)
    stacked = jnp.concatenate([past_frames, activated], axis=0)
    extended = extended_2(stacked, (("span", 1),), 1)
    padded = jnp.pad(extended, ((0, 0), (0, 0), (1, 1), (0, 0)))
    frame_count = frames.shape[0]
    rows_here = frames.shape[1]
    col_count = frames.shape[2]
    channels = frames.shape[3]
    windows = []
    for frame_tap in range(3):
        for row_tap in range(3):
            for col_tap in range(3):
                windows.append(
                    padded[
                        frame_tap : frame_tap + frame_count,
                        row_tap : row_tap + rows_here,
                        col_tap : col_tap + col_count,
                        :,
                    ]
                )
    columns = jnp.concatenate(windows, axis=-1).reshape(-1, 27 * channels)
    convolved = jnp.dot(
        columns, conv_weight.reshape(27 * channels, channels), preferred_element_type=jnp.float32
    )
    decoded = features + conv_bias + convolved.reshape(frame_count, rows_here, col_count, channels)
    return (attended, decoded.astype(jnp.bfloat16))


def solution(mesh):
    placed = (
        P(("group", "span"), None),
        P(None, ("group", "span"), None),
        P("group"),
        P("group", None),
        P("group"),
        P("group", "span", None, None),
        P("group", "span", None, None),
        P(),
        P(),
        P(),
    )
    return jax.shard_map(
        shards,
        mesh=mesh,
        in_specs=placed,
        out_specs=(P(("group", "span"), None), P("group", "span", None, None)),
        check_vma=False,
    )
```
